128 devices in a mesh: rad: 8 (over y, core), mode: 16 (over z, x).
Axes of the slice: x: 4, y: 4, z: 4, core: 2. Of those that a mesh axis runs over, the one named last changes fastest.
Arguments:
- spectra: bfloat16 [2, 256, 1024, 1024], P(None, 'mode', 'rad'), may hold values from -6 to 6
- diffusivity: float32 [1024], replicated, may hold values from 0.1 to 1
- eigenvalues: float32 [1024], replicated, may hold values from 0.3 to 3
- radial_basis: bfloat16 [1024, 1024], replicated, may hold values from -0.1875 to 0.1875
- dual_basis: bfloat16 [1024, 1024], replicated, may hold values from -0.1875 to 0.1875
- degree_count: int32 [256], replicated, may hold values from 1 to 1024, as said below
- order_slot: int32 [256], replicated, may hold values from 0 to 255, as said below
Outputs:
- stepped: bfloat16 [2, 256, 1024, 1024], P(None, 'mode', 'rad')
The draws below stay inside these ranges and needn't reach their ends.
Inputs may be any that keep to these rules, and one draw needn't show every extreme that they name: `degree_count`: row i holds order m_i = floor(i * 2); at most 1024 - m_i of its slots are live, and row 0 has all 1024. `order_slot`: A permutation of the rows. Output row d * 16 + s + k takes an input row of block s, that is one of s * 16 to (s + 1) * 16 - 1.
All inputs are finite; a program needn't handle non-finite values.
Results may differ from the reference program's by a relative error of at most 0.0065.
Values may be sent and summed in bfloat16 or wider, within the bound.
No kernel may reach another device: no remote copies, remote signals or barrier semaphores. Data moves between devices by JAX's collectives and lax.ppermute only.
A program may use at most 192 MiB of HBM per device.

```python
import math
import jax
import jax.numpy as jnp
from jax import lax

NR = 1024
L = 1024
ORD_DEV = 16
NM = 256
SHARE = 1
N_MODE = 16


def draw_degree_count(key, part):
    row_ids = jnp.arange(NM, dtype=jnp.int32)
    orders = row_ids * L // (2 * NM)
    trimmed = jax.random.randint(key, (NM,), 0, L // 16, dtype=jnp.int32)
    trimmed = jnp.where(row_ids == 0, 0, trimmed)
    return (L - orders - trimmed).astype(jnp.int32)


def draw_order_slot(key, part):
    source_keys = jax.random.split(jax.random.fold_in(key, 7), N_MODE)
    orderings = jax.vmap(lambda sub_key: jax.random.permutation(sub_key, ORD_DEV))(source_keys)
    orderings = orderings.astype(jnp.int32).reshape(N_MODE, N_MODE, SHARE)
    offsets = (jnp.arange(N_MODE, dtype=jnp.int32) * ORD_DEV)[:, None, None]
    chosen = orderings + offsets
    return jnp.transpose(chosen, (1, 0, 2)).reshape(NM).astype(jnp.int32)


def levels(key, shape, pieces, least, high):
    def one(dim, parts):
        steps = jax.random.uniform(jax.random.fold_in(jax.random.fold_in(key, 6), dim), (parts,), jnp.float32, least / len(pieces), high / len(pieces))
        return jnp.repeat(jnp.exp(steps), shape[dim] // parts).reshape((-1,) + (1,) * (len(shape) - dim - 1))

    gain = one(*pieces[0])
    for cut in pieces[1:]:
        gain = gain * one(*cut)
    return gain


def gaussian(own_key, extent, deviation, most, cuts=(), kind=jnp.bfloat16):
    loudness = levels(own_key, extent, cuts, -0.22, 0.18) if cuts else 1.0
    result = jax.random.normal(own_key, extent, jnp.float32) * deviation * loudness
    return jnp.minimum(jnp.maximum(result, -most), most).astype(kind)


def setup_inputs(seed: int = 0) -> dict:
    arg_keys = jax.random.split(jax.random.key(seed), 8)
    spectra = gaussian(arg_keys[0], (2, NM, NR, L), 1.0, 6.0, ((1, 16), (2, 8)))
    diffusivity = jnp.clip(jnp.exp(jax.random.uniform(arg_keys[1], (NR,), jnp.float32, math.log(0.1), math.log(1.0))), 0.1, 1.0)
    eigenvalues = jnp.clip(jnp.exp(jax.random.uniform(arg_keys[2], (NR,), jnp.float32, math.log(0.3), math.log(3.0))), 0.3, 3.0)
    radial_basis = gaussian(arg_keys[3], (NR, NR), NR ** -0.5, 0.1875)
    dual_basis = gaussian(arg_keys[4], (NR, NR), NR ** -0.5, 0.1875)
    degree_count = draw_degree_count(jax.random.fold_in(arg_keys[7], 71), 0)
    order_slot = draw_order_slot(jax.random.fold_in(arg_keys[7], 71), 0)
    return {"spectra": spectra, "diffusivity": diffusivity, "eigenvalues": eigenvalues, "radial_basis": radial_basis, "dual_basis": dual_basis, "degree_count": degree_count, "order_slot": order_slot}


def degree_table(counts, order_start, order_rows, slot_start, slot_width, slots_total, orders_total):
    row_ids = order_start + jnp.arange(order_rows, dtype=jnp.int32)
    orders = (row_ids * slots_total) // (2 * orders_total)
    slot_ids = slot_start + jnp.arange(slot_width, dtype=jnp.int32)
    degree = (orders[:, None] + slot_ids[None, :]).astype(jnp.float32)
    limits = lax.dynamic_slice_in_dim(counts, order_start, order_rows)
    live_mask = slot_ids[None, :] < limits[:, None]
    return degree, live_mask


def explicit(padded, kappa_rows, radius_start, degree, live_mask, shells_total):
    center = padded[:, :, 2:-2]
    shell_rows = center.shape[2]
    second = (-padded[:, :, :-4] + 16.0 * padded[:, :, 1:-3] - 30.0 * center
              + 16.0 * padded[:, :, 3:-1] - padded[:, :, 4:]) / 12.0
    radius = 1.2 + (radius_start + jnp.arange(shell_rows, dtype=jnp.int32)).astype(jnp.float32) / shells_total
    damping = (degree * (degree + 1.0))[None, :, None, :] / ((shells_total * radius) ** 2)[None, None, :, None]
    updated = center + 0.5 * kappa_rows[None, None, :, None] * (second - damping * center)
    return jnp.where(live_mask[None, :, None, :], updated, 0.0).astype(jnp.bfloat16)


def reference(spectra, diffusivity, eigenvalues, radial_basis, dual_basis, degree_count, order_slot):
    orders_total = spectra.shape[1]
    shells_total = spectra.shape[2]
    slots_total = spectra.shape[3]
    block = math.gcd(orders_total, 16)
    identity = jnp.eye(shells_total, dtype=jnp.float32)
    basis_full = (identity + radial_basis.astype(jnp.float32)).astype(jnp.bfloat16)
    dual_full = (identity + dual_basis.astype(jnp.float32)).astype(jnp.bfloat16)
    basis_full = lax.optimization_barrier(basis_full).astype(jnp.float32)
    dual_full = lax.optimization_barrier(dual_full).astype(jnp.float32)

    def one_block(block_index):
        start = (block_index * block).astype(jnp.int32)
        piece = lax.dynamic_slice_in_dim(spectra, start, block, 1).astype(jnp.float32)
        degree, live_mask = degree_table(degree_count, start, block, 0, slots_total, slots_total, orders_total)
        padded = jnp.pad(piece, ((0, 0), (0, 0), (2, 2), (0, 0)))
        updated = explicit(padded, diffusivity, 0, degree, live_mask, shells_total)
        updated = lax.optimization_barrier(updated).astype(jnp.float32)
        projected = jnp.einsum('kr,cirj->cikj', dual_full, updated)
        divisor = eigenvalues[None, None, :, None] + 0.5 * (degree * (degree + 1.0))[None, :, None, :] / (shells_total * shells_total)
        scaled = (projected / divisor).astype(jnp.bfloat16)
        scaled = lax.optimization_barrier(scaled).astype(jnp.float32)
        restored = jnp.einsum('kr,cirj->cikj', basis_full, scaled)
        return jnp.where(live_mask[None, :, None, :], restored, 0.0).astype(jnp.bfloat16)

    stacked = lax.map(one_block, jnp.arange(orders_total // block, dtype=jnp.int32))
    solved = jnp.moveaxis(stacked, 0, 1).reshape(2, orders_total, shells_total, slots_total)
    return jnp.take(solved, order_slot, axis=1)
```

```python
import jax
import jax.numpy as jnp
from jax import lax
from jax.sharding import PartitionSpec as P


def explicit(padded, kappa_rows, radius_start, degree, live_mask, shells_total):
    center = padded[:, :, 2:-2]
    shell_rows = center.shape[2]
    second = (
        -padded[:, :, :-4]
        + 16.0 * padded[:, :, 1:-3]
        - 30.0 * center
        + 16.0 * padded[:, :, 3:-1]
        - padded[:, :, 4:]
    ) / 12.0
    radius = (
        1.2
        + (radius_start + jnp.arange(shell_rows, dtype=jnp.int32)).astype(jnp.float32)
        / shells_total
    )
    damping = (degree * (degree + 1.0))[None, :, None, :] / ((shells_total * radius) ** 2)[
        None, None, :, None
    ]
    updated = center + 0.5 * kappa_rows[None, None, :, None] * (second - damping * center)
    return jnp.where(live_mask[None, :, None, :], updated, 0.0).astype(jnp.bfloat16)


def on_device(
    spectra, diffusivity, eigenvalues, radial_basis, dual_basis, degree_count, order_slot
):
    comps, rows_here, shells_here, slots_total = spectra.shape
    shells_total = diffusivity.shape[0]
    orders_total = degree_count.shape[0]
    groups = lax.axis_size("mode")
    nrad = lax.axis_size("rad")
    per_group = rows_here // groups
    window = slots_total // nrad
    me_mode = lax.axis_index("mode")
    me_rad = lax.axis_index("rad")

    picks = (
        lax.dynamic_slice_in_dim(
            order_slot.reshape(groups, groups, per_group), me_mode, 1, 1
        ).reshape(groups * per_group)
        - me_mode * rows_here
    )
    chosen = jnp.take(spectra, picks, axis=1)
    send = chosen.reshape(comps, groups, per_group, shells_here, nrad, window)
    send = send.transpose(1, 4, 0, 2, 3, 5).reshape(
        groups * nrad, comps, per_group, shells_here, window
    )
    recv = lax.all_to_all(send, ("mode", "rad"), 0, 0, tiled=True)
    local = recv.reshape(groups, nrad, comps, per_group, shells_here, window)
    local = local.transpose(2, 0, 3, 1, 4, 5).reshape(comps, rows_here, shells_total, window)

    out_rows = me_mode * rows_here + jnp.arange(rows_here, dtype=jnp.int32)
    in_rows = jnp.take(order_slot, out_rows)
    orders = in_rows * slots_total // (2 * orders_total)
    slot_ids = me_rad * window + jnp.arange(window, dtype=jnp.int32)
    degree = (orders[:, None] + slot_ids[None, :]).astype(jnp.float32)
    live = slot_ids[None, :] < jnp.take(degree_count, in_rows)[:, None]

    padded = jnp.pad(local.astype(jnp.float32), ((0, 0), (0, 0), (2, 2), (0, 0)))
    updated = explicit(padded, diffusivity, 0, degree, live, shells_total)

    identity = jnp.eye(shells_total, dtype=jnp.float32)
    basis_full = (identity + radial_basis.astype(jnp.float32)).astype(jnp.bfloat16)
    dual_full = (identity + dual_basis.astype(jnp.float32)).astype(jnp.bfloat16)
    projected = jnp.einsum("kr,cirj->cikj", dual_full, updated, preferred_element_type=jnp.float32)
    divisor = eigenvalues[None, None, :, None] + 0.5 * (degree * (degree + 1.0))[
        None, :, None, :
    ] / (shells_total * shells_total)
    scaled = (projected / divisor).astype(jnp.bfloat16)
    restored = jnp.einsum("kr,cirj->cikj", basis_full, scaled, preferred_element_type=jnp.float32)
    solved = jnp.where(live[None, :, None, :], restored, 0.0).astype(jnp.bfloat16)

    back = solved.reshape(comps, rows_here, nrad, shells_here, window).transpose(2, 0, 1, 3, 4)
    got = lax.all_to_all(back, "rad", 0, 0, tiled=True)
    return got.transpose(1, 2, 3, 0, 4).reshape(comps, rows_here, shells_here, slots_total)


def solution(mesh):
    placed = (P(None, "mode", "rad", None), P(), P(), P(), P(), P(), P())
    return jax.shard_map(
        on_device,
        mesh=mesh,
        in_specs=placed,
        out_specs=P(None, "mode", "rad", None),
        check_vma=False,
    )
```

```python
import functools

import jax
import jax.numpy as jnp
from jax import lax
from jax.experimental import pallas as pl
from jax.experimental.pallas import tpu as pltpu
from jax.sharding import PartitionSpec as P

PAD = 8


def pack_kernel(picks_ref, x_ref, o_ref):
    nrad, window = o_ref.shape[0], o_ref.shape[-1]
    for w in range(nrad):
        o_ref[w, 0, 0] = x_ref[0, 0, :, w * window:(w + 1) * window]


def pack(spectra, picks, groups, nrad, per_group):
    comps, rows_here, shells_here, slots_total = spectra.shape
    window = slots_total // nrad
    return pl.pallas_call(
        pack_kernel,
        out_shape=jax.ShapeDtypeStruct(
            (groups * nrad, comps, per_group, shells_here, window), spectra.dtype
        ),
        grid_spec=pltpu.PrefetchScalarGridSpec(
            num_scalar_prefetch=1,
            grid=(groups * per_group, comps),
            in_specs=[
                pl.BlockSpec(
                    (1, 1, shells_here, slots_total), lambda q, c, p: (c, p[q], 0, 0)
                )
            ],
            out_specs=pl.BlockSpec(
                (nrad, 1, 1, shells_here, window),
                lambda q, c, p: (q // per_group, c, q % per_group, 0, 0),
            ),
        ),
    )(picks, spectra)


def solve_kernel(x_ref, info_ref, kappa_ref, invden_ref, eig_ref, d_ref, b_ref, o_ref, pad_ref):
    nrad, comps = x_ref.shape[1], x_ref.shape[2]
    sh, window = x_ref.shape[4], x_ref.shape[5]
    nr = nrad * sh
    cols = [x_ref[0, :, c, 0].reshape(nr, window) for c in range(comps)]
    f = jnp.concatenate(cols, axis=1).astype(jnp.float32)
    width = f.shape[1]
    pad_ref[0:PAD, :] = jnp.zeros((PAD, width), jnp.float32)
    pad_ref[PAD + nr:PAD + nr + PAD, :] = jnp.zeros((PAD, width), jnp.float32)
    pad_ref[PAD:PAD + nr, :] = f
    m2 = pad_ref[PAD - 2:PAD - 2 + nr, :]
    m1 = pad_ref[PAD - 1:PAD - 1 + nr, :]
    p1 = pad_ref[PAD + 1:PAD + 1 + nr, :]
    p2 = pad_ref[PAD + 2:PAD + 2 + nr, :]
    second = (-m2 + 16.0 * m1 - 30.0 * f + 16.0 * p1 - p2) / 12.0
    deg = info_ref[0, 0:1, :]
    live = info_ref[0, 1:2, :] > 0.5
    lterm = deg * (deg + 1.0)
    damping = lterm * invden_ref[...]
    updated = f + 0.5 * kappa_ref[...] * (second - damping * f)
    updated = jnp.where(live, updated, 0.0).astype(jnp.bfloat16)
    projected = jnp.dot(d_ref[...], updated, preferred_element_type=jnp.float32)
    divisor = eig_ref[...] + 0.5 * lterm / float(nr * nr)
    scaled = (projected / divisor).astype(jnp.bfloat16)
    restored = jnp.dot(b_ref[...], scaled, preferred_element_type=jnp.float32)
    solved = jnp.where(live, restored, 0.0).astype(jnp.bfloat16)
    for c in range(comps):
        o_ref[:, c, 0] = solved[:, c * window:(c + 1) * window].reshape(nrad, sh, window)


def solve(recv, info, kappa, invden, eig, dual_full, basis_full, groups, nrad, per_group):
    _, comps, _, sh, window = recv.shape
    nr = nrad * sh
    rows_here = groups * per_group
    x = recv.reshape(groups, nrad, comps, per_group, sh, window)
    width = comps * window
    flops = 2 * 2 * nr * nr * width * rows_here
    return pl.pallas_call(
        solve_kernel,
        out_shape=jax.ShapeDtypeStruct((nrad, comps, rows_here, sh, window), jnp.bfloat16),
        grid=(rows_here,),
        in_specs=[
            pl.BlockSpec(
                (1, nrad, comps, 1, sh, window),
                lambda q: (q // per_group, 0, 0, q % per_group, 0, 0),
            ),
            pl.BlockSpec((1, 8, width), lambda q: (q, 0, 0)),
            pl.BlockSpec((nr, 1), lambda q: (0, 0)),
            pl.BlockSpec((nr, 1), lambda q: (0, 0)),
            pl.BlockSpec((nr, 1), lambda q: (0, 0)),
            pl.BlockSpec((nr, nr), lambda q: (0, 0)),
            pl.BlockSpec((nr, nr), lambda q: (0, 0)),
        ],
        out_specs=pl.BlockSpec((nrad, comps, 1, sh, window), lambda q: (0, 0, q, 0, 0)),
        scratch_shapes=[pltpu.VMEM((nr + 2 * PAD, width), jnp.float32)],
        compiler_params=pltpu.CompilerParams(vmem_limit_bytes=48 * 1024 * 1024),
        cost_estimate=pl.CostEstimate(
            flops=flops, transcendentals=0, bytes_accessed=4 * recv.size + 4 * nr * nr
        ),
    )(x, info, kappa, invden, eig, dual_full, basis_full)


def unpack_kernel(x_ref, o_ref):
    nrad, window = x_ref.shape[0], x_ref.shape[-1]
    for w in range(nrad):
        o_ref[0, 0, :, w * window:(w + 1) * window] = x_ref[w, 0, 0]


def unpack(got):
    nrad, comps, rows_here, sh, window = got.shape
    return pl.pallas_call(
        unpack_kernel,
        out_shape=jax.ShapeDtypeStruct((comps, rows_here, sh, nrad * window), got.dtype),
        grid=(comps, rows_here),
        in_specs=[pl.BlockSpec((nrad, 1, 1, sh, window), lambda c, r: (0, c, r, 0, 0))],
        out_specs=pl.BlockSpec((1, 1, sh, nrad * window), lambda c, r: (c, r, 0, 0)),
    )(got)


def on_device(
    spectra, diffusivity, eigenvalues, radial_basis, dual_basis, degree_count, order_slot
):
    comps, rows_here, shells_here, slots_total = spectra.shape
    shells_total = diffusivity.shape[0]
    orders_total = degree_count.shape[0]
    groups = lax.axis_size("mode")
    nrad = lax.axis_size("rad")
    per_group = rows_here // groups
    window = slots_total // nrad
    me_mode = lax.axis_index("mode")
    me_rad = lax.axis_index("rad")

    picks = (
        lax.dynamic_slice_in_dim(
            order_slot.reshape(groups, groups, per_group), me_mode, 1, 1
        ).reshape(groups * per_group)
        - me_mode * rows_here
    )
    send = pack(spectra, picks, groups, nrad, per_group)
    recv = lax.all_to_all(send, ("mode", "rad"), 0, 0, tiled=True)

    out_rows = me_mode * rows_here + jnp.arange(rows_here, dtype=jnp.int32)
    in_rows = jnp.take(order_slot, out_rows)
    orders = in_rows * slots_total // (2 * orders_total)
    slot_ids = me_rad * window + jnp.arange(window, dtype=jnp.int32)
    degree = (orders[:, None] + slot_ids[None, :]).astype(jnp.float32)
    live = (slot_ids[None, :] < jnp.take(degree_count, in_rows)[:, None]).astype(jnp.float32)
    info = jnp.zeros((rows_here, 8, comps * window), jnp.float32)
    info = info.at[:, 0, :].set(jnp.tile(degree, (1, comps)))
    info = info.at[:, 1, :].set(jnp.tile(live, (1, comps)))

    radius = 1.2 + jnp.arange(shells_total, dtype=jnp.int32).astype(jnp.float32) / shells_total
    invden = (1.0 / ((shells_total * radius) ** 2)).reshape(shells_total, 1)
    kappa = diffusivity.reshape(shells_total, 1)
    eig = eigenvalues.reshape(shells_total, 1)

    identity = jnp.eye(shells_total, dtype=jnp.float32)
    basis_full = (identity + radial_basis.astype(jnp.float32)).astype(jnp.bfloat16)
    dual_full = (identity + dual_basis.astype(jnp.float32)).astype(jnp.bfloat16)
    back = solve(recv, info, kappa, invden, eig, dual_full, basis_full, groups, nrad, per_group)
    got = lax.all_to_all(back, "rad", 0, 0, tiled=True)
    return unpack(got)


def solution(mesh):
    placed = (P(None, "mode", "rad", None), P(), P(), P(), P(), P(), P())
    return jax.shard_map(
        on_device,
        mesh=mesh,
        in_specs=placed,
        out_specs=P(None, "mode", "rad", None),
        check_vma=False,
    )
```

```python
import functools

import jax
import jax.numpy as jnp
from jax import lax
from jax.experimental import pallas as pl
from jax.experimental.pallas import tpu as pltpu
from jax.sharding import PartitionSpec as P

PAD = 8


def pack_kernel(picks_ref, *refs):
    x_refs, o_ref = refs[:-1], refs[-1]
    nrad, window = o_ref.shape[0] // len(x_refs), o_ref.shape[-1]
    for i, x_ref in enumerate(x_refs):
        for w in range(nrad):
            o_ref[i * nrad + w] = x_ref[:, 0:1, :, w * window:(w + 1) * window]


def pack(spectra, picks, groups, nrad, per_group, step=4):
    comps, rows_here, shells_here, slots_total = spectra.shape
    window = slots_total // nrad
    picks_total = groups * per_group

    def in_map(i):
        return lambda q, p: (0, p[q * step + i], 0, 0)

    def out_map(q, p):
        return (q, 0, 0, 0, 0)

    assert per_group == 1 and picks_total % step == 0
    return pl.pallas_call(
        pack_kernel,
        out_shape=jax.ShapeDtypeStruct(
            (groups * nrad, comps, per_group, shells_here, window), spectra.dtype
        ),
        grid_spec=pltpu.PrefetchScalarGridSpec(
            num_scalar_prefetch=1,
            grid=(picks_total // step,),
            in_specs=[
                pl.BlockSpec((comps, 1, shells_here, slots_total), in_map(i))
                for i in range(step)
            ],
            out_specs=pl.BlockSpec(
                (step * nrad, comps, per_group, shells_here, window), out_map
            ),
        ),
    )(picks, *([spectra] * step))


def solve_kernel(x_ref, info_ref, kappa_ref, invden_ref, eig_ref, d_ref, b_ref, o_ref, pad_ref):
    nrad, comps = x_ref.shape[1], x_ref.shape[2]
    sh, window = x_ref.shape[4], x_ref.shape[5]
    nr = nrad * sh
    cols = [x_ref[0, :, c, 0].reshape(nr, window) for c in range(comps)]
    f = jnp.concatenate(cols, axis=1).astype(jnp.float32)
    width = f.shape[1]
    pad_ref[0:PAD, :] = jnp.zeros((PAD, width), jnp.float32)
    pad_ref[PAD + nr:PAD + nr + PAD, :] = jnp.zeros((PAD, width), jnp.float32)
    pad_ref[PAD:PAD + nr, :] = f
    m2 = pad_ref[PAD - 2:PAD - 2 + nr, :]
    m1 = pad_ref[PAD - 1:PAD - 1 + nr, :]
    p1 = pad_ref[PAD + 1:PAD + 1 + nr, :]
    p2 = pad_ref[PAD + 2:PAD + 2 + nr, :]
    second = (-m2 + 16.0 * m1 - 30.0 * f + 16.0 * p1 - p2) / 12.0
    deg = info_ref[0, 0:1, :]
    live = info_ref[0, 1:2, :] > 0.5
    lterm = deg * (deg + 1.0)
    damping = lterm * invden_ref[...]
    updated = f + 0.5 * kappa_ref[...] * (second - damping * f)
    updated = jnp.where(live, updated, 0.0).astype(jnp.bfloat16)
    projected = jnp.dot(d_ref[...], updated, preferred_element_type=jnp.float32)
    divisor = eig_ref[...] + 0.5 * lterm / float(nr * nr)
    scaled = (projected / divisor).astype(jnp.bfloat16)
    restored = jnp.dot(b_ref[...], scaled, preferred_element_type=jnp.float32)
    solved = jnp.where(live, restored, 0.0).astype(jnp.bfloat16)
    for c in range(comps):
        o_ref[:, c, 0] = solved[:, c * window:(c + 1) * window].reshape(nrad, sh, window)


def solve(recv, info, kappa, invden, eig, dual_full, basis_full, groups, nrad, per_group):
    _, comps, _, sh, window = recv.shape
    nr = nrad * sh
    rows_here = groups * per_group
    x = recv.reshape(groups, nrad, comps, per_group, sh, window)
    width = comps * window
    flops = 2 * 2 * nr * nr * width * rows_here
    return pl.pallas_call(
        solve_kernel,
        out_shape=jax.ShapeDtypeStruct((nrad, comps, rows_here, sh, window), jnp.bfloat16),
        grid=(rows_here,),
        in_specs=[
            pl.BlockSpec(
                (1, nrad, comps, 1, sh, window),
                lambda q: (q // per_group, 0, 0, q % per_group, 0, 0),
            ),
            pl.BlockSpec((1, 8, width), lambda q: (q, 0, 0)),
            pl.BlockSpec((nr, 1), lambda q: (0, 0)),
            pl.BlockSpec((nr, 1), lambda q: (0, 0)),
            pl.BlockSpec((nr, 1), lambda q: (0, 0)),
            pl.BlockSpec((nr, nr), lambda q: (0, 0)),
            pl.BlockSpec((nr, nr), lambda q: (0, 0)),
        ],
        out_specs=pl.BlockSpec((nrad, comps, 1, sh, window), lambda q: (0, 0, q, 0, 0)),
        scratch_shapes=[pltpu.VMEM((nr + 2 * PAD, width), jnp.float32)],
        compiler_params=pltpu.CompilerParams(vmem_limit_bytes=48 * 1024 * 1024),
        cost_estimate=pl.CostEstimate(
            flops=flops, transcendentals=0, bytes_accessed=4 * recv.size + 4 * nr * nr
        ),
    )(x, info, kappa, invden, eig, dual_full, basis_full)


def unpack_kernel(x_ref, o_ref):
    nrad, window = x_ref.shape[0], x_ref.shape[-1]
    for w in range(nrad):
        o_ref[:, :, :, w * window:(w + 1) * window] = x_ref[w]


def unpack(got, step=4):
    nrad, comps, rows_here, sh, window = got.shape
    return pl.pallas_call(
        unpack_kernel,
        out_shape=jax.ShapeDtypeStruct((comps, rows_here, sh, nrad * window), got.dtype),
        grid=(rows_here // step,),
        in_specs=[pl.BlockSpec((nrad, comps, step, sh, window), lambda r: (0, 0, r, 0, 0))],
        out_specs=pl.BlockSpec((comps, step, sh, nrad * window), lambda r: (0, r, 0, 0)),
    )(got)


def on_device(
    spectra, diffusivity, eigenvalues, radial_basis, dual_basis, degree_count, order_slot
):
    comps, rows_here, shells_here, slots_total = spectra.shape
    shells_total = diffusivity.shape[0]
    orders_total = degree_count.shape[0]
    groups = lax.axis_size("mode")
    nrad = lax.axis_size("rad")
    per_group = rows_here // groups
    window = slots_total // nrad
    me_mode = lax.axis_index("mode")
    me_rad = lax.axis_index("rad")

    picks = (
        lax.dynamic_slice_in_dim(
            order_slot.reshape(groups, groups, per_group), me_mode, 1, 1
        ).reshape(groups * per_group)
        - me_mode * rows_here
    )
    send = pack(spectra, picks, groups, nrad, per_group)
    recv = lax.all_to_all(send, ("mode", "rad"), 0, 0, tiled=True)

    out_rows = me_mode * rows_here + jnp.arange(rows_here, dtype=jnp.int32)
    in_rows = jnp.take(order_slot, out_rows)
    orders = in_rows * slots_total // (2 * orders_total)
    slot_ids = me_rad * window + jnp.arange(window, dtype=jnp.int32)
    degree = (orders[:, None] + slot_ids[None, :]).astype(jnp.float32)
    live = (slot_ids[None, :] < jnp.take(degree_count, in_rows)[:, None]).astype(jnp.float32)
    info = jnp.zeros((rows_here, 8, comps * window), jnp.float32)
    info = info.at[:, 0, :].set(jnp.tile(degree, (1, comps)))
    info = info.at[:, 1, :].set(jnp.tile(live, (1, comps)))

    radius = 1.2 + jnp.arange(shells_total, dtype=jnp.int32).astype(jnp.float32) / shells_total
    invden = (1.0 / ((shells_total * radius) ** 2)).reshape(shells_total, 1)
    kappa = diffusivity.reshape(shells_total, 1)
    eig = eigenvalues.reshape(shells_total, 1)

    identity = jnp.eye(shells_total, dtype=jnp.float32)
    basis_full = (identity + radial_basis.astype(jnp.float32)).astype(jnp.bfloat16)
    dual_full = (identity + dual_basis.astype(jnp.float32)).astype(jnp.bfloat16)
    back = solve(recv, info, kappa, invden, eig, dual_full, basis_full, groups, nrad, per_group)
    got = lax.all_to_all(back, "rad", 0, 0, tiled=True)
    return unpack(got)


def solution(mesh):
    placed = (P(None, "mode", "rad", None), P(), P(), P(), P(), P(), P())
    return jax.shard_map(
        on_device,
        mesh=mesh,
        in_specs=placed,
        out_specs=P(None, "mode", "rad", None),
        check_vma=False,
    )
```

```python
import functools

import jax
import jax.numpy as jnp
from jax import lax
from jax.experimental import pallas as pl
from jax.experimental.pallas import tpu as pltpu
from jax.sharding import PartitionSpec as P

PAD = 8


def pack_kernel(picks_ref, *refs):
    x_refs, o_ref = refs[:-1], refs[-1]
    nrad, window = o_ref.shape[0] // len(x_refs), o_ref.shape[-1]
    for i, x_ref in enumerate(x_refs):
        for w in range(nrad):
            o_ref[i * nrad + w] = x_ref[:, 0:1, :, w * window:(w + 1) * window]


def pack(spectra, picks, comp, groups, nrad, per_group, step=4):
    comps, rows_here, shells_here, slots_total = spectra.shape
    window = slots_total // nrad
    picks_total = groups * per_group

    def in_map(i):
        return lambda q, p: (comp, p[q * step + i], 0, 0)

    def out_map(q, p):
        return (q, 0, 0, 0, 0)

    assert per_group == 1 and picks_total % step == 0
    return pl.pallas_call(
        pack_kernel,
        out_shape=jax.ShapeDtypeStruct(
            (groups * nrad, 1, per_group, shells_here, window), spectra.dtype
        ),
        grid_spec=pltpu.PrefetchScalarGridSpec(
            num_scalar_prefetch=1,
            grid=(picks_total // step,),
            in_specs=[
                pl.BlockSpec((1, 1, shells_here, slots_total), in_map(i))
                for i in range(step)
            ],
            out_specs=pl.BlockSpec((step * nrad, 1, per_group, shells_here, window), out_map),
        ),
    )(picks, *([spectra] * step))


def solve_kernel(x_ref, info_ref, kappa_ref, invden_ref, eig_ref, d_ref, b_ref, o_ref, pad_ref):
    npos, nrad = x_ref.shape[0], x_ref.shape[1]
    sh, window = x_ref.shape[4], x_ref.shape[5]
    nr = nrad * sh
    cols = [x_ref[j, :, 0, 0].reshape(nr, window) for j in range(npos)]
    f = jnp.concatenate(cols, axis=1).astype(jnp.float32)
    width = f.shape[1]
    pad_ref[0:PAD, :] = jnp.zeros((PAD, width), jnp.float32)
    pad_ref[PAD + nr:PAD + nr + PAD, :] = jnp.zeros((PAD, width), jnp.float32)
    pad_ref[PAD:PAD + nr, :] = f
    m2 = pad_ref[PAD - 2:PAD - 2 + nr, :]
    m1 = pad_ref[PAD - 1:PAD - 1 + nr, :]
    p1 = pad_ref[PAD + 1:PAD + 1 + nr, :]
    p2 = pad_ref[PAD + 2:PAD + 2 + nr, :]
    second = (-m2 + 16.0 * m1 - 30.0 * f + 16.0 * p1 - p2) / 12.0
    deg = jnp.concatenate([info_ref[j, 0:1, :] for j in range(npos)], axis=1)
    live = jnp.concatenate([info_ref[j, 1:2, :] for j in range(npos)], axis=1) > 0.5
    lterm = deg * (deg + 1.0)
    damping = lterm * invden_ref[...]
    updated = f + 0.5 * kappa_ref[...] * (second - damping * f)
    updated = jnp.where(live, updated, 0.0).astype(jnp.bfloat16)
    projected = jnp.dot(d_ref[...], updated, preferred_element_type=jnp.float32)
    divisor = eig_ref[...] + 0.5 * lterm / float(nr * nr)
    scaled = (projected / divisor).astype(jnp.bfloat16)
    restored = jnp.dot(b_ref[...], scaled, preferred_element_type=jnp.float32)
    solved = jnp.where(live, restored, 0.0).astype(jnp.bfloat16)
    for j in range(npos):
        o_ref[:, 0, j] = solved[:, j * window:(j + 1) * window].reshape(nrad, sh, window)


def solve(recv, info, kappa, invden, eig, dual_full, basis_full, groups, nrad, per_group, npos=2):
    _, _, _, sh, window = recv.shape
    nr = nrad * sh
    rows_here = groups * per_group
    assert per_group == 1 and rows_here % npos == 0
    x = recv.reshape(groups, nrad, 1, per_group, sh, window)
    width = npos * window
    flops = 2 * 2 * nr * nr * window * rows_here
    return pl.pallas_call(
        solve_kernel,
        out_shape=jax.ShapeDtypeStruct((nrad, 1, rows_here, sh, window), jnp.bfloat16),
        grid=(rows_here // npos,),
        in_specs=[
            pl.BlockSpec((npos, nrad, 1, 1, sh, window), lambda q: (q, 0, 0, 0, 0, 0)),
            pl.BlockSpec((npos, 8, window), lambda q: (q, 0, 0)),
            pl.BlockSpec((nr, 1), lambda q: (0, 0)),
            pl.BlockSpec((nr, 1), lambda q: (0, 0)),
            pl.BlockSpec((nr, 1), lambda q: (0, 0)),
            pl.BlockSpec((nr, nr), lambda q: (0, 0)),
            pl.BlockSpec((nr, nr), lambda q: (0, 0)),
        ],
        out_specs=pl.BlockSpec((nrad, 1, npos, sh, window), lambda q: (0, 0, q, 0, 0)),
        scratch_shapes=[pltpu.VMEM((nr + 2 * PAD, width), jnp.float32)],
        compiler_params=pltpu.CompilerParams(vmem_limit_bytes=48 * 1024 * 1024),
        cost_estimate=pl.CostEstimate(
            flops=flops, transcendentals=0, bytes_accessed=4 * recv.size + 4 * nr * nr
        ),
    )(x, info, kappa, invden, eig, dual_full, basis_full)


def unpack_kernel(*refs):
    x_refs, o_ref = refs[:-1], refs[-1]
    nrad, window = x_refs[0].shape[0], x_refs[0].shape[-1]
    for c, x_ref in enumerate(x_refs):
        for w in range(nrad):
            o_ref[c, :, :, w * window:(w + 1) * window] = x_ref[w, 0]


def unpack(gots, step=4):
    nrad, _, rows_here, sh, window = gots[0].shape
    comps = len(gots)
    return pl.pallas_call(
        unpack_kernel,
        out_shape=jax.ShapeDtypeStruct((comps, rows_here, sh, nrad * window), gots[0].dtype),
        grid=(rows_here // step,),
        in_specs=[
            pl.BlockSpec((nrad, 1, step, sh, window), lambda r: (0, 0, r, 0, 0))
            for _ in gots
        ],
        out_specs=pl.BlockSpec((comps, step, sh, nrad * window), lambda r: (0, r, 0, 0)),
    )(*gots)


def on_device(
    spectra, diffusivity, eigenvalues, radial_basis, dual_basis, degree_count, order_slot
):
    comps, rows_here, shells_here, slots_total = spectra.shape
    shells_total = diffusivity.shape[0]
    orders_total = degree_count.shape[0]
    groups = lax.axis_size("mode")
    nrad = lax.axis_size("rad")
    per_group = rows_here // groups
    window = slots_total // nrad
    me_mode = lax.axis_index("mode")
    me_rad = lax.axis_index("rad")

    picks = (
        lax.dynamic_slice_in_dim(
            order_slot.reshape(groups, groups, per_group), me_mode, 1, 1
        ).reshape(groups * per_group)
        - me_mode * rows_here
    )
    recvs = []
    for comp in range(comps):
        send = pack(spectra, picks, comp, groups, nrad, per_group)
        recvs.append(lax.all_to_all(send, ("mode", "rad"), 0, 0, tiled=True))

    out_rows = me_mode * rows_here + jnp.arange(rows_here, dtype=jnp.int32)
    in_rows = jnp.take(order_slot, out_rows)
    orders = in_rows * slots_total // (2 * orders_total)
    slot_ids = me_rad * window + jnp.arange(window, dtype=jnp.int32)
    degree = (orders[:, None] + slot_ids[None, :]).astype(jnp.float32)
    live = (slot_ids[None, :] < jnp.take(degree_count, in_rows)[:, None]).astype(jnp.float32)
    info = jnp.zeros((rows_here, 8, window), jnp.float32)
    info = info.at[:, 0, :].set(degree)
    info = info.at[:, 1, :].set(live)

    radius = 1.2 + jnp.arange(shells_total, dtype=jnp.int32).astype(jnp.float32) / shells_total
    invden = (1.0 / ((shells_total * radius) ** 2)).reshape(shells_total, 1)
    kappa = diffusivity.reshape(shells_total, 1)
    eig = eigenvalues.reshape(shells_total, 1)

    identity = jnp.eye(shells_total, dtype=jnp.float32)
    basis_full = (identity + radial_basis.astype(jnp.float32)).astype(jnp.bfloat16)
    dual_full = (identity + dual_basis.astype(jnp.float32)).astype(jnp.bfloat16)
    gots = []
    for recv in recvs:
        back = solve(recv, info, kappa, invden, eig, dual_full, basis_full, groups, nrad, per_group)
        gots.append(lax.all_to_all(back, "rad", 0, 0, tiled=True))
    return unpack(gots)


def solution(mesh):
    placed = (P(None, "mode", "rad", None), P(), P(), P(), P(), P(), P())
    return jax.shard_map(
        on_device,
        mesh=mesh,
        in_specs=placed,
        out_specs=P(None, "mode", "rad", None),
        check_vma=False,
    )
```

```python
import functools

import jax
import jax.numpy as jnp
from jax import lax
from jax.experimental import pallas as pl
from jax.experimental.pallas import tpu as pltpu
from jax.sharding import PartitionSpec as P

PAD = 8


def layout_tables(groups, nrad, rows_here, slots_total, orders_total):
    window = slots_total // nrad
    nwin = []
    for s in range(groups):
        least = (s * rows_here) * slots_total // (2 * orders_total)
        nwin.append(max(1, min(nrad, -(-(slots_total - least) // window))))
    load = [0] * nrad
    shift = [0] * groups
    for s in sorted(range(groups), key=lambda s: nwin[s]):
        best = None
        for sh in range(nrad):
            trial = load[:]
            for w in range(nwin[s], nrad):
                trial[(w + sh) % nrad] += 1
            key = (max(trial), sum(x * x for x in trial))
            if best is None or key < best[0]:
                best = (key, sh, trial)
        shift[s], load = best[1], best[2]
    lists = []
    for r in range(nrad):
        lists.append([s for s in range(groups) if (r - shift[s]) % nrad < nwin[s]])
    count = max(len(x) for x in lists)
    pos_tab, win_tab, ok_tab = [], [], []
    for r in range(nrad):
        entries = lists[r] + [lists[r][0]] * (count - len(lists[r]))
        pos_tab.append(entries)
        win_tab.append([(r - shift[s]) % nrad for s in entries])
        ok_tab.append([1] * len(lists[r]) + [0] * (count - len(lists[r])))
    src_r, src_j, src_ok = [], [], []
    for s in range(groups):
        for w in range(nrad):
            r = (w + shift[s]) % nrad
            live = w < nwin[s]
            src_r.append(r)
            src_j.append(lists[r].index(s) if live else 0)
            src_ok.append(1 if live else 0)
    dest_tab = [[(w + shift[s]) % nrad for w in range(nrad)] for s in range(groups)]
    return dict(count=count, pos=pos_tab, win=win_tab, ok=ok_tab, src_r=src_r, src_j=src_j,
                src_ok=src_ok, dest=dest_tab)


def pack_kernel(picks_ref, dest_ref, *refs):
    x_refs, o_ref = refs[:-1], refs[-1]
    nrad, window = o_ref.shape[0] // len(x_refs), o_ref.shape[-1]
    for i, x_ref in enumerate(x_refs):
        for w in range(nrad):
            o_ref[i * nrad + dest_ref[w]] = x_ref[:, 0:1, :, w * window:(w + 1) * window]


def pack(spectra, picks, dests, comp, groups, nrad, per_group, step=4):
    comps, rows_here, shells_here, slots_total = spectra.shape
    window = slots_total // nrad
    picks_total = groups * per_group

    def in_map(i):
        return lambda q, p, d: (comp, p[q * step + i], 0, 0)

    def out_map(q, p, d):
        return (q, 0, 0, 0, 0)

    assert per_group == 1 and picks_total % step == 0
    return pl.pallas_call(
        pack_kernel,
        out_shape=jax.ShapeDtypeStruct(
            (groups * nrad, 1, per_group, shells_here, window), spectra.dtype
        ),
        grid_spec=pltpu.PrefetchScalarGridSpec(
            num_scalar_prefetch=2,
            grid=(picks_total // step,),
            in_specs=[
                pl.BlockSpec((1, 1, shells_here, slots_total), in_map(i))
                for i in range(step)
            ],
            out_specs=pl.BlockSpec((step * nrad, 1, per_group, shells_here, window), out_map),
        ),
    )(picks, dests, *([spectra] * step))


def solve_kernel(pos_ref, x_ref, info_ref, kappa_ref, invden_ref, eig_ref, d_ref, b_ref, o_ref,
                 pad_ref):
    nrad = x_ref.shape[1]
    sh, window = x_ref.shape[4], x_ref.shape[5]
    nr = nrad * sh
    f = x_ref[0, :, 0, 0].reshape(nr, window).astype(jnp.float32)
    width = f.shape[1]
    pad_ref[0:PAD, :] = jnp.zeros((PAD, width), jnp.float32)
    pad_ref[PAD + nr:PAD + nr + PAD, :] = jnp.zeros((PAD, width), jnp.float32)
    pad_ref[PAD:PAD + nr, :] = f
    m2 = pad_ref[PAD - 2:PAD - 2 + nr, :]
    m1 = pad_ref[PAD - 1:PAD - 1 + nr, :]
    p1 = pad_ref[PAD + 1:PAD + 1 + nr, :]
    p2 = pad_ref[PAD + 2:PAD + 2 + nr, :]
    second = (-m2 + 16.0 * m1 - 30.0 * f + 16.0 * p1 - p2) / 12.0
    deg = info_ref[0, 0:1, :]
    live = info_ref[0, 1:2, :] > 0.5
    lterm = deg * (deg + 1.0)
    damping = lterm * invden_ref[...]
    updated = f + 0.5 * kappa_ref[...] * (second - damping * f)
    updated = jnp.where(live, updated, 0.0).astype(jnp.bfloat16)
    projected = jnp.dot(d_ref[...], updated, preferred_element_type=jnp.float32)
    divisor = eig_ref[...] + 0.5 * lterm / float(nr * nr)
    scaled = (projected / divisor).astype(jnp.bfloat16)
    restored = jnp.dot(b_ref[...], scaled, preferred_element_type=jnp.float32)
    solved = jnp.where(live, restored, 0.0).astype(jnp.bfloat16)
    o_ref[:, 0, 0] = solved.reshape(nrad, sh, window)


def solve(recv, pos, info, kappa, invden, eig, dual_full, basis_full, groups, nrad, per_group):
    _, _, _, sh, window = recv.shape
    nr = nrad * sh
    count = pos.shape[0]
    assert per_group == 1
    x = recv.reshape(groups, nrad, 1, per_group, sh, window)
    flops = 2 * 2 * nr * nr * window * count
    return pl.pallas_call(
        solve_kernel,
        out_shape=jax.ShapeDtypeStruct((nrad, 1, count, sh, window), jnp.bfloat16),
        grid_spec=pltpu.PrefetchScalarGridSpec(
            num_scalar_prefetch=1,
            grid=(count,),
            in_specs=[
                pl.BlockSpec((1, nrad, 1, 1, sh, window), lambda q, p: (p[q], 0, 0, 0, 0, 0)),
                pl.BlockSpec((1, 8, window), lambda q, p: (q, 0, 0)),
                pl.BlockSpec((nr, 1), lambda q, p: (0, 0)),
                pl.BlockSpec((nr, 1), lambda q, p: (0, 0)),
                pl.BlockSpec((nr, 1), lambda q, p: (0, 0)),
                pl.BlockSpec((nr, nr), lambda q, p: (0, 0)),
                pl.BlockSpec((nr, nr), lambda q, p: (0, 0)),
            ],
            out_specs=pl.BlockSpec((nrad, 1, 1, sh, window), lambda q, p: (0, 0, q, 0, 0)),
            scratch_shapes=[pltpu.VMEM((nr + 2 * PAD, window), jnp.float32)],
        ),
        compiler_params=pltpu.CompilerParams(vmem_limit_bytes=48 * 1024 * 1024),
        cost_estimate=pl.CostEstimate(
            flops=flops, transcendentals=0, bytes_accessed=4 * count * nr * window + 4 * nr * nr
        ),
    )(pos, x, info, kappa, invden, eig, dual_full, basis_full)


def unpack_kernel(r_ref, j_ref, ok_ref, *refs):
    x_refs, o_ref = refs[:-1], refs[-1]
    nrad, window = x_refs[0].shape[0], x_refs[0].shape[-1]
    s = pl.program_id(0)
    for c, x_ref in enumerate(x_refs):
        for w in range(nrad):
            k = s * nrad + w
            blk = x_ref[r_ref[k], 0, j_ref[k]]
            o_ref[c, 0, :, w * window:(w + 1) * window] = jnp.where(
                ok_ref[k] > 0, blk, jnp.zeros_like(blk)
            )


def unpack(gots, src_r, src_j, src_ok, rows_here):
    nrad, _, count, sh, window = gots[0].shape
    comps = len(gots)
    return pl.pallas_call(
        unpack_kernel,
        out_shape=jax.ShapeDtypeStruct((comps, rows_here, sh, nrad * window), gots[0].dtype),
        grid_spec=pltpu.PrefetchScalarGridSpec(
            num_scalar_prefetch=3,
            grid=(rows_here,),
            in_specs=[
                pl.BlockSpec((nrad, 1, count, sh, window), lambda s, a, b, c: (0, 0, 0, 0, 0))
                for _ in gots
            ],
            out_specs=pl.BlockSpec(
                (comps, 1, sh, nrad * window), lambda s, a, b, c: (0, s, 0, 0)
            ),
        ),
        compiler_params=pltpu.CompilerParams(vmem_limit_bytes=48 * 1024 * 1024),
    )(src_r, src_j, src_ok, *gots)


def on_device(
    spectra, diffusivity, eigenvalues, radial_basis, dual_basis, degree_count, order_slot
):
    comps, rows_here, shells_here, slots_total = spectra.shape
    shells_total = diffusivity.shape[0]
    orders_total = degree_count.shape[0]
    groups = lax.axis_size("mode")
    nrad = lax.axis_size("rad")
    per_group = rows_here // groups
    window = slots_total // nrad
    me_mode = lax.axis_index("mode")
    me_rad = lax.axis_index("rad")
    tab = layout_tables(groups, nrad, rows_here, slots_total, orders_total)

    picks = (
        lax.dynamic_slice_in_dim(
            order_slot.reshape(groups, groups, per_group), me_mode, 1, 1
        ).reshape(groups * per_group)
        - me_mode * rows_here
    )
    dests = jnp.asarray(tab["dest"], jnp.int32)[me_mode]
    recvs = []
    for comp in range(comps):
        send = pack(spectra, picks, dests, comp, groups, nrad, per_group)
        recvs.append(lax.all_to_all(send, ("mode", "rad"), 0, 0, tiled=True))

    pos = jnp.asarray(tab["pos"], jnp.int32)[me_rad]
    win = jnp.asarray(tab["win"], jnp.int32)[me_rad]
    ok = jnp.asarray(tab["ok"], jnp.int32)[me_rad]
    in_rows = jnp.take(order_slot, me_mode * rows_here + pos)
    orders = in_rows * slots_total // (2 * orders_total)
    slot_ids = win[:, None] * window + jnp.arange(window, dtype=jnp.int32)[None, :]
    degree = (orders[:, None] + slot_ids).astype(jnp.float32)
    live = (slot_ids < jnp.take(degree_count, in_rows)[:, None]) & (ok[:, None] > 0)
    count = tab["count"]
    info = jnp.zeros((count, 8, window), jnp.float32)
    info = info.at[:, 0, :].set(degree)
    info = info.at[:, 1, :].set(live.astype(jnp.float32))

    radius = 1.2 + jnp.arange(shells_total, dtype=jnp.int32).astype(jnp.float32) / shells_total
    invden = (1.0 / ((shells_total * radius) ** 2)).reshape(shells_total, 1)
    kappa = diffusivity.reshape(shells_total, 1)
    eig = eigenvalues.reshape(shells_total, 1)

    identity = jnp.eye(shells_total, dtype=jnp.float32)
    basis_full = (identity + radial_basis.astype(jnp.float32)).astype(jnp.bfloat16)
    dual_full = (identity + dual_basis.astype(jnp.float32)).astype(jnp.bfloat16)
    gots = []
    for recv in recvs:
        back = solve(recv, pos, info, kappa, invden, eig, dual_full, basis_full, groups, nrad,
                     per_group)
        gots.append(lax.all_to_all(back, "rad", 0, 0, tiled=True))
    src_r = jnp.asarray(tab["src_r"], jnp.int32)
    src_j = jnp.asarray(tab["src_j"], jnp.int32)
    src_ok = jnp.asarray(tab["src_ok"], jnp.int32)
    return unpack(gots, src_r, src_j, src_ok, rows_here)


def solution(mesh):
    placed = (P(None, "mode", "rad", None), P(), P(), P(), P(), P(), P())
    return jax.shard_map(
        on_device,
        mesh=mesh,
        in_specs=placed,
        out_specs=P(None, "mode", "rad", None),
        check_vma=False,
    )
```

```python
import functools

import jax
import jax.numpy as jnp
from jax import lax
from jax.experimental import pallas as pl
from jax.experimental.pallas import tpu as pltpu
from jax.sharding import PartitionSpec as P

PAD = 8


def layout_tables(groups, nrad, rows_here, slots_total, orders_total):
    window = slots_total // nrad
    nwin = []
    for s in range(groups):
        least = (s * rows_here) * slots_total // (2 * orders_total)
        nwin.append(max(1, min(nrad, -(-(slots_total - least) // window))))
    load = [0] * nrad
    shift = [0] * groups
    for s in sorted(range(groups), key=lambda s: nwin[s]):
        best = None
        for sh in range(nrad):
            trial = load[:]
            for w in range(nwin[s], nrad):
                trial[(w + sh) % nrad] += 1
            key = (max(trial), sum(x * x for x in trial))
            if best is None or key < best[0]:
                best = (key, sh, trial)
        shift[s], load = best[1], best[2]
    lists = []
    for r in range(nrad):
        lists.append([s for s in range(groups) if (r - shift[s]) % nrad < nwin[s]])
    count = max(len(x) for x in lists)
    count += count % 2
    pos_tab, win_tab, ok_tab = [], [], []
    for r in range(nrad):
        entries = lists[r] + [lists[r][0]] * (count - len(lists[r]))
        pos_tab.append(entries)
        win_tab.append([(r - shift[s]) % nrad for s in entries])
        ok_tab.append([1] * len(lists[r]) + [0] * (count - len(lists[r])))
    src_r, src_j, src_ok = [], [], []
    for s in range(groups):
        for w in range(nrad):
            r = (w + shift[s]) % nrad
            live = w < nwin[s]
            src_r.append(r)
            src_j.append(lists[r].index(s) if live else 0)
            src_ok.append(1 if live else 0)
    dest_tab = [[(w + shift[s]) % nrad for w in range(nrad)] for s in range(groups)]
    return dict(count=count, pos=pos_tab, win=win_tab, ok=ok_tab, src_r=src_r, src_j=src_j,
                src_ok=src_ok, dest=dest_tab)


def pack_kernel(picks_ref, dest_ref, *refs):
    x_refs, o_ref = refs[:-1], refs[-1]
    nrad, window = o_ref.shape[0] // len(x_refs), o_ref.shape[-1]
    for i, x_ref in enumerate(x_refs):
        for w in range(nrad):
            o_ref[i * nrad + dest_ref[w]] = x_ref[:, 0:1, :, w * window:(w + 1) * window]


def pack(spectra, picks, dests, comp, groups, nrad, per_group, step=4):
    comps, rows_here, shells_here, slots_total = spectra.shape
    window = slots_total // nrad
    picks_total = groups * per_group

    def in_map(i):
        return lambda q, p, d: (comp, p[q * step + i], 0, 0)

    def out_map(q, p, d):
        return (q, 0, 0, 0, 0)

    assert per_group == 1 and picks_total % step == 0
    return pl.pallas_call(
        pack_kernel,
        out_shape=jax.ShapeDtypeStruct(
            (groups * nrad, 1, per_group, shells_here, window), spectra.dtype
        ),
        grid_spec=pltpu.PrefetchScalarGridSpec(
            num_scalar_prefetch=2,
            grid=(picks_total // step,),
            in_specs=[
                pl.BlockSpec((1, 1, shells_here, slots_total), in_map(i))
                for i in range(step)
            ],
            out_specs=pl.BlockSpec((step * nrad, 1, per_group, shells_here, window), out_map),
        ),
    )(picks, dests, *([spectra] * step))


def solve_kernel(pos_ref, *refs):
    npos = len(refs) - 8
    x_refs = refs[:npos]
    info_ref, kappa_ref, invden_ref, eig_ref, d_ref, b_ref, o_ref, pad_ref = refs[npos:]
    nrad = x_refs[0].shape[1]
    sh, window = x_refs[0].shape[4], x_refs[0].shape[5]
    nr = nrad * sh
    cols = [x_ref[0, :, 0, 0].reshape(nr, window) for x_ref in x_refs]
    f = jnp.concatenate(cols, axis=1).astype(jnp.float32)
    width = f.shape[1]
    pad_ref[0:PAD, :] = jnp.zeros((PAD, width), jnp.float32)
    pad_ref[PAD + nr:PAD + nr + PAD, :] = jnp.zeros((PAD, width), jnp.float32)
    pad_ref[PAD:PAD + nr, :] = f
    m2 = pad_ref[PAD - 2:PAD - 2 + nr, :]
    m1 = pad_ref[PAD - 1:PAD - 1 + nr, :]
    p1 = pad_ref[PAD + 1:PAD + 1 + nr, :]
    p2 = pad_ref[PAD + 2:PAD + 2 + nr, :]
    second = (-m2 + 16.0 * m1 - 30.0 * f + 16.0 * p1 - p2) / 12.0
    deg = jnp.concatenate([info_ref[j, 0:1, :] for j in range(npos)], axis=1)
    live = jnp.concatenate([info_ref[j, 1:2, :] for j in range(npos)], axis=1) > 0.5
    lterm = deg * (deg + 1.0)
    damping = lterm * invden_ref[...]
    updated = f + 0.5 * kappa_ref[...] * (second - damping * f)
    updated = jnp.where(live, updated, 0.0).astype(jnp.bfloat16)
    projected = jnp.dot(d_ref[...], updated, preferred_element_type=jnp.float32)
    divisor = eig_ref[...] + 0.5 * lterm / float(nr * nr)
    scaled = (projected / divisor).astype(jnp.bfloat16)
    restored = jnp.dot(b_ref[...], scaled, preferred_element_type=jnp.float32)
    solved = jnp.where(live, restored, 0.0).astype(jnp.bfloat16)
    for j in range(npos):
        o_ref[:, 0, j] = solved[:, j * window:(j + 1) * window].reshape(nrad, sh, window)


def solve(recv, pos, info, kappa, invden, eig, dual_full, basis_full, groups, nrad, per_group,
          npos=2):
    _, _, _, sh, window = recv.shape
    nr = nrad * sh
    count = pos.shape[0]
    assert per_group == 1 and count % npos == 0
    x = recv.reshape(groups, nrad, 1, per_group, sh, window)
    flops = 2 * 2 * nr * nr * window * count

    def x_map(j):
        return lambda q, p: (p[q * npos + j], 0, 0, 0, 0, 0)

    return pl.pallas_call(
        solve_kernel,
        out_shape=jax.ShapeDtypeStruct((nrad, 1, count, sh, window), jnp.bfloat16),
        grid_spec=pltpu.PrefetchScalarGridSpec(
            num_scalar_prefetch=1,
            grid=(count // npos,),
            in_specs=[
                pl.BlockSpec((1, nrad, 1, 1, sh, window), x_map(j)) for j in range(npos)
            ] + [
                pl.BlockSpec((npos, 8, window), lambda q, p: (q, 0, 0)),
                pl.BlockSpec((nr, 1), lambda q, p: (0, 0)),
                pl.BlockSpec((nr, 1), lambda q, p: (0, 0)),
                pl.BlockSpec((nr, 1), lambda q, p: (0, 0)),
                pl.BlockSpec((nr, nr), lambda q, p: (0, 0)),
                pl.BlockSpec((nr, nr), lambda q, p: (0, 0)),
            ],
            out_specs=pl.BlockSpec((nrad, 1, npos, sh, window), lambda q, p: (0, 0, q, 0, 0)),
            scratch_shapes=[pltpu.VMEM((nr + 2 * PAD, npos * window), jnp.float32)],
        ),
        compiler_params=pltpu.CompilerParams(vmem_limit_bytes=48 * 1024 * 1024),
        cost_estimate=pl.CostEstimate(
            flops=flops, transcendentals=0, bytes_accessed=4 * count * nr * window + 4 * nr * nr
        ),
    )(pos, *([x] * npos), info, kappa, invden, eig, dual_full, basis_full)


def unpack_kernel(r_ref, j_ref, ok_ref, x_ref, *refs):
    o_ref = refs[-1]
    nrad, window = x_ref.shape[0], x_ref.shape[-1]
    s = pl.program_id(0)
    for w in range(nrad):
        k = s * nrad + w
        blk = x_ref[r_ref[k], 0, j_ref[k]]
        o_ref[0, 0, :, w * window:(w + 1) * window] = jnp.where(
            ok_ref[k] > 0, blk, jnp.zeros_like(blk)
        )


def unpack(got, comp, comps, prev, src_r, src_j, src_ok, rows_here):
    nrad, _, count, sh, window = got.shape
    shape = (comps, rows_here, sh, nrad * window)
    in_specs = [pl.BlockSpec((nrad, 1, count, sh, window), lambda s, a, b, c: (0, 0, 0, 0, 0))]
    args = [got]
    aliases = {}
    if prev is not None:
        in_specs.append(pl.BlockSpec(memory_space=pl.ANY))
        args.append(prev)
        aliases = {4: 0}
    return pl.pallas_call(
        unpack_kernel,
        out_shape=jax.ShapeDtypeStruct(shape, got.dtype),
        grid_spec=pltpu.PrefetchScalarGridSpec(
            num_scalar_prefetch=3,
            grid=(rows_here,),
            in_specs=in_specs,
            out_specs=pl.BlockSpec(
                (1, 1, sh, nrad * window), lambda s, a, b, c: (comp, s, 0, 0)
            ),
        ),
        input_output_aliases=aliases,
        compiler_params=pltpu.CompilerParams(vmem_limit_bytes=48 * 1024 * 1024),
    )(src_r, src_j, src_ok, *args)


def on_device(
    spectra, diffusivity, eigenvalues, radial_basis, dual_basis, degree_count, order_slot
):
    comps, rows_here, shells_here, slots_total = spectra.shape
    shells_total = diffusivity.shape[0]
    orders_total = degree_count.shape[0]
    groups = lax.axis_size("mode")
    nrad = lax.axis_size("rad")
    per_group = rows_here // groups
    window = slots_total // nrad
    me_mode = lax.axis_index("mode")
    me_rad = lax.axis_index("rad")
    tab = layout_tables(groups, nrad, rows_here, slots_total, orders_total)

    picks = (
        lax.dynamic_slice_in_dim(
            order_slot.reshape(groups, groups, per_group), me_mode, 1, 1
        ).reshape(groups * per_group)
        - me_mode * rows_here
    )
    dests = jnp.asarray(tab["dest"], jnp.int32)[me_mode]
    recvs = []
    for comp in range(comps):
        send = pack(spectra, picks, dests, comp, groups, nrad, per_group)
        recvs.append(lax.all_to_all(send, ("mode", "rad"), 0, 0, tiled=True))

    pos = jnp.asarray(tab["pos"], jnp.int32)[me_rad]
    win = jnp.asarray(tab["win"], jnp.int32)[me_rad]
    ok = jnp.asarray(tab["ok"], jnp.int32)[me_rad]
    in_rows = jnp.take(order_slot, me_mode * rows_here + pos)
    orders = in_rows * slots_total // (2 * orders_total)
    slot_ids = win[:, None] * window + jnp.arange(window, dtype=jnp.int32)[None, :]
    degree = (orders[:, None] + slot_ids).astype(jnp.float32)
    live = (slot_ids < jnp.take(degree_count, in_rows)[:, None]) & (ok[:, None] > 0)
    count = tab["count"]
    info = jnp.zeros((count, 8, window), jnp.float32)
    info = info.at[:, 0, :].set(degree)
    info = info.at[:, 1, :].set(live.astype(jnp.float32))

    radius = 1.2 + jnp.arange(shells_total, dtype=jnp.int32).astype(jnp.float32) / shells_total
    invden = (1.0 / ((shells_total * radius) ** 2)).reshape(shells_total, 1)
    kappa = diffusivity.reshape(shells_total, 1)
    eig = eigenvalues.reshape(shells_total, 1)

    identity = jnp.eye(shells_total, dtype=jnp.float32)
    basis_full = (identity + radial_basis.astype(jnp.float32)).astype(jnp.bfloat16)
    dual_full = (identity + dual_basis.astype(jnp.float32)).astype(jnp.bfloat16)
    gots = []
    for recv in recvs:
        back = solve(recv, pos, info, kappa, invden, eig, dual_full, basis_full, groups, nrad,
                     per_group)
        gots.append(lax.all_to_all(back, "rad", 0, 0, tiled=True))
    src_r = jnp.asarray(tab["src_r"], jnp.int32)
    src_j = jnp.asarray(tab["src_j"], jnp.int32)
    src_ok = jnp.asarray(tab["src_ok"], jnp.int32)
    out = None
    for comp, got in enumerate(gots):
        out = unpack(got, comp, comps, out, src_r, src_j, src_ok, rows_here)
    return out


def solution(mesh):
    placed = (P(None, "mode", "rad", None), P(), P(), P(), P(), P(), P())
    return jax.shard_map(
        on_device,
        mesh=mesh,
        in_specs=placed,
        out_specs=P(None, "mode", "rad", None),
        check_vma=False,
    )
```

```python
import functools

import jax
import jax.numpy as jnp
from jax import lax
from jax.experimental import pallas as pl
from jax.experimental.pallas import tpu as pltpu
from jax.sharding import PartitionSpec as P

PAD = 8


def layout_tables(groups, nrad, rows_here, slots_total, orders_total):
    window = slots_total // nrad
    nwin = []
    for s in range(groups):
        least = (s * rows_here) * slots_total // (2 * orders_total)
        nwin.append(max(1, min(nrad, -(-(slots_total - least) // window))))
    load = [0] * nrad
    shift = [0] * groups
    for s in sorted(range(groups), key=lambda s: nwin[s]):
        best = None
        for sh in range(nrad):
            trial = load[:]
            for w in range(nwin[s], nrad):
                trial[(w + sh) % nrad] += 1
            key = (max(trial), sum(x * x for x in trial))
            if best is None or key < best[0]:
                best = (key, sh, trial)
        shift[s], load = best[1], best[2]
    lists = []
    for r in range(nrad):
        lists.append([s for s in range(groups) if (r - shift[s]) % nrad < nwin[s]])
    count = max(len(x) for x in lists)
    pos_tab, win_tab, ok_tab = [], [], []
    for r in range(nrad):
        entries = lists[r] + [lists[r][0]] * (count - len(lists[r]))
        pos_tab.append(entries)
        win_tab.append([(r - shift[s]) % nrad for s in entries])
        ok_tab.append([1] * len(lists[r]) + [0] * (count - len(lists[r])))
    src_r, src_j, src_ok = [], [], []
    for s in range(groups):
        for w in range(nrad):
            r = (w + shift[s]) % nrad
            live = w < nwin[s]
            src_r.append(r)
            src_j.append(lists[r].index(s) if live else 0)
            src_ok.append(1 if live else 0)
    dest_tab = [[(w + shift[s]) % nrad for w in range(nrad)] for s in range(groups)]
    return dict(count=count, pos=pos_tab, win=win_tab, ok=ok_tab, src_r=src_r, src_j=src_j,
                src_ok=src_ok, dest=dest_tab)


def pack_kernel(picks_ref, dest_ref, *refs):
    x_refs, o_ref = refs[:-1], refs[-1]
    nrad, window = o_ref.shape[0] // len(x_refs), o_ref.shape[-1]
    for i, x_ref in enumerate(x_refs):
        for w in range(nrad):
            o_ref[i * nrad + dest_ref[w]] = x_ref[:, 0:1, :, w * window:(w + 1) * window]


def pack(spectra, picks, dests, comp, groups, nrad, per_group, step=4):
    comps, rows_here, shells_here, slots_total = spectra.shape
    window = slots_total // nrad
    picks_total = groups * per_group

    def in_map(i):
        return lambda q, p, d: (comp, p[q * step + i], 0, 0)

    def out_map(q, p, d):
        return (q, 0, 0, 0, 0)

    assert per_group == 1 and picks_total % step == 0
    return pl.pallas_call(
        pack_kernel,
        out_shape=jax.ShapeDtypeStruct(
            (groups * nrad, 1, per_group, shells_here, window), spectra.dtype
        ),
        grid_spec=pltpu.PrefetchScalarGridSpec(
            num_scalar_prefetch=2,
            grid=(picks_total // step,),
            in_specs=[
                pl.BlockSpec((1, 1, shells_here, slots_total), in_map(i))
                for i in range(step)
            ],
            out_specs=pl.BlockSpec((step * nrad, 1, per_group, shells_here, window), out_map),
        ),
    )(picks, dests, *([spectra] * step))


def solve_kernel(pos_ref, *refs):
    npos = len(refs) - 8
    x_refs = refs[:npos]
    info_ref, kappa_ref, invden_ref, eig_ref, d_ref, b_ref, o_ref, pad_ref = refs[npos:]
    nrad = x_refs[0].shape[1]
    sh, window = x_refs[0].shape[4], x_refs[0].shape[5]
    nr = nrad * sh
    cols = [x_ref[0, :, 0, 0].reshape(nr, window) for x_ref in x_refs]
    f = jnp.concatenate(cols, axis=1).astype(jnp.float32)
    width = f.shape[1]
    pad_ref[0:PAD, :] = jnp.zeros((PAD, width), jnp.float32)
    pad_ref[PAD + nr:PAD + nr + PAD, :] = jnp.zeros((PAD, width), jnp.float32)
    pad_ref[PAD:PAD + nr, :] = f
    m2 = pad_ref[PAD - 2:PAD - 2 + nr, :]
    m1 = pad_ref[PAD - 1:PAD - 1 + nr, :]
    p1 = pad_ref[PAD + 1:PAD + 1 + nr, :]
    p2 = pad_ref[PAD + 2:PAD + 2 + nr, :]
    second = (-m2 + 16.0 * m1 - 30.0 * f + 16.0 * p1 - p2) / 12.0
    deg = jnp.concatenate([info_ref[j, 0:1, :] for j in range(npos)], axis=1)
    live = jnp.concatenate([info_ref[j, 1:2, :] for j in range(npos)], axis=1) > 0.5
    lterm = deg * (deg + 1.0)
    damping = lterm * invden_ref[...]
    updated = f + 0.5 * kappa_ref[...] * (second - damping * f)
    updated = jnp.where(live, updated, 0.0).astype(jnp.bfloat16)
    projected = jnp.dot(d_ref[...], updated, preferred_element_type=jnp.float32)
    divisor = eig_ref[...] + 0.5 * lterm / float(nr * nr)
    scaled = (projected / divisor).astype(jnp.bfloat16)
    restored = jnp.dot(b_ref[...], scaled, preferred_element_type=jnp.float32)
    solved = jnp.where(live, restored, 0.0).astype(jnp.bfloat16)
    for j in range(npos):
        o_ref[:, 0, j] = solved[:, j * window:(j + 1) * window].reshape(nrad, sh, window)


def solve(recv, pos, info, kappa, invden, eig, dual_full, basis_full, groups, nrad, per_group,
          npos=1):
    _, _, _, sh, window = recv.shape
    nr = nrad * sh
    count = pos.shape[0]
    assert per_group == 1 and count % npos == 0
    x = recv.reshape(groups, nrad, 1, per_group, sh, window)
    flops = 2 * 2 * nr * nr * window * count

    def x_map(j):
        return lambda q, p: (p[q * npos + j], 0, 0, 0, 0, 0)

    return pl.pallas_call(
        solve_kernel,
        out_shape=jax.ShapeDtypeStruct((nrad, 1, count, sh, window), jnp.bfloat16),
        grid_spec=pltpu.PrefetchScalarGridSpec(
            num_scalar_prefetch=1,
            grid=(count // npos,),
            in_specs=[
                pl.BlockSpec((1, nrad, 1, 1, sh, window), x_map(j)) for j in range(npos)
            ] + [
                pl.BlockSpec((npos, 8, window), lambda q, p: (q, 0, 0)),
                pl.BlockSpec((nr, 1), lambda q, p: (0, 0)),
                pl.BlockSpec((nr, 1), lambda q, p: (0, 0)),
                pl.BlockSpec((nr, 1), lambda q, p: (0, 0)),
                pl.BlockSpec((nr, nr), lambda q, p: (0, 0)),
                pl.BlockSpec((nr, nr), lambda q, p: (0, 0)),
            ],
            out_specs=pl.BlockSpec((nrad, 1, npos, sh, window), lambda q, p: (0, 0, q, 0, 0)),
            scratch_shapes=[pltpu.VMEM((nr + 2 * PAD, npos * window), jnp.float32)],
        ),
        compiler_params=pltpu.CompilerParams(vmem_limit_bytes=48 * 1024 * 1024),
        cost_estimate=pl.CostEstimate(
            flops=flops, transcendentals=0, bytes_accessed=4 * count * nr * window + 4 * nr * nr
        ),
    )(pos, *([x] * npos), info, kappa, invden, eig, dual_full, basis_full)


def unpack_kernel(r_ref, j_ref, ok_ref, x_ref, *refs):
    o_ref = refs[-1]
    nrad, window = x_ref.shape[0], x_ref.shape[-1]
    step = o_ref.shape[1]
    s = pl.program_id(0)
    for i in range(step):
        for w in range(nrad):
            k = (s * step + i) * nrad + w
            blk = x_ref[r_ref[k], 0, j_ref[k]]
            o_ref[0, i, :, w * window:(w + 1) * window] = jnp.where(
                ok_ref[k] > 0, blk, jnp.zeros_like(blk)
            )


def unpack(got, comp, comps, prev, src_r, src_j, src_ok, rows_here, step=4):
    nrad, _, count, sh, window = got.shape
    shape = (comps, rows_here, sh, nrad * window)
    in_specs = [pl.BlockSpec((nrad, 1, count, sh, window), lambda s, a, b, c: (0, 0, 0, 0, 0))]
    args = [got]
    aliases = {}
    if prev is not None:
        in_specs.append(pl.BlockSpec(memory_space=pl.ANY))
        args.append(prev)
        aliases = {4: 0}
    return pl.pallas_call(
        unpack_kernel,
        out_shape=jax.ShapeDtypeStruct(shape, got.dtype),
        grid_spec=pltpu.PrefetchScalarGridSpec(
            num_scalar_prefetch=3,
            grid=(rows_here // step,),
            in_specs=in_specs,
            out_specs=pl.BlockSpec(
                (1, step, sh, nrad * window), lambda s, a, b, c: (comp, s, 0, 0)
            ),
        ),
        input_output_aliases=aliases,
        compiler_params=pltpu.CompilerParams(vmem_limit_bytes=48 * 1024 * 1024),
    )(src_r, src_j, src_ok, *args)


def on_device(
    spectra, diffusivity, eigenvalues, radial_basis, dual_basis, degree_count, order_slot
):
    comps, rows_here, shells_here, slots_total = spectra.shape
    shells_total = diffusivity.shape[0]
    orders_total = degree_count.shape[0]
    groups = lax.axis_size("mode")
    nrad = lax.axis_size("rad")
    per_group = rows_here // groups
    window = slots_total // nrad
    me_mode = lax.axis_index("mode")
    me_rad = lax.axis_index("rad")
    tab = layout_tables(groups, nrad, rows_here, slots_total, orders_total)

    picks = (
        lax.dynamic_slice_in_dim(
            order_slot.reshape(groups, groups, per_group), me_mode, 1, 1
        ).reshape(groups * per_group)
        - me_mode * rows_here
    )
    dests = jnp.asarray(tab["dest"], jnp.int32)[me_mode]
    recvs = []
    for comp in range(comps):
        send = pack(spectra, picks, dests, comp, groups, nrad, per_group)
        recvs.append(lax.all_to_all(send, ("mode", "rad"), 0, 0, tiled=True))

    pos = jnp.asarray(tab["pos"], jnp.int32)[me_rad]
    win = jnp.asarray(tab["win"], jnp.int32)[me_rad]
    ok = jnp.asarray(tab["ok"], jnp.int32)[me_rad]
    in_rows = jnp.take(order_slot, me_mode * rows_here + pos)
    orders = in_rows * slots_total // (2 * orders_total)
    slot_ids = win[:, None] * window + jnp.arange(window, dtype=jnp.int32)[None, :]
    degree = (orders[:, None] + slot_ids).astype(jnp.float32)
    live = (slot_ids < jnp.take(degree_count, in_rows)[:, None]) & (ok[:, None] > 0)
    count = tab["count"]
    info = jnp.zeros((count, 8, window), jnp.float32)
    info = info.at[:, 0, :].set(degree)
    info = info.at[:, 1, :].set(live.astype(jnp.float32))

    radius = 1.2 + jnp.arange(shells_total, dtype=jnp.int32).astype(jnp.float32) / shells_total
    invden = (1.0 / ((shells_total * radius) ** 2)).reshape(shells_total, 1)
    kappa = diffusivity.reshape(shells_total, 1)
    eig = eigenvalues.reshape(shells_total, 1)

    identity = jnp.eye(shells_total, dtype=jnp.float32)
    basis_full = (identity + radial_basis.astype(jnp.float32)).astype(jnp.bfloat16)
    dual_full = (identity + dual_basis.astype(jnp.float32)).astype(jnp.bfloat16)
    gots = []
    for recv in recvs:
        back = solve(recv, pos, info, kappa, invden, eig, dual_full, basis_full, groups, nrad,
                     per_group)
        gots.append(lax.all_to_all(back, "rad", 0, 0, tiled=True))
    src_r = jnp.asarray(tab["src_r"], jnp.int32)
    src_j = jnp.asarray(tab["src_j"], jnp.int32)
    src_ok = jnp.asarray(tab["src_ok"], jnp.int32)
    out = None
    for comp, got in enumerate(gots):
        out = unpack(got, comp, comps, out, src_r, src_j, src_ok, rows_here)
    return out


def solution(mesh):
    placed = (P(None, "mode", "rad", None), P(), P(), P(), P(), P(), P())
    return jax.shard_map(
        on_device,
        mesh=mesh,
        in_specs=placed,
        out_specs=P(None, "mode", "rad", None),
        check_vma=False,
    )
```

```python
import functools

import jax
import jax.numpy as jnp
from jax import lax
from jax.experimental import pallas as pl
from jax.experimental.pallas import tpu as pltpu
from jax.sharding import PartitionSpec as P

PAD = 8
SPLIT = 4


def layout_tables(groups, nrad, rows_here, slots_total, orders_total):
    window = slots_total // nrad
    nwin = []
    for s in range(groups):
        least = (s * rows_here) * slots_total // (2 * orders_total)
        nwin.append(max(1, min(nrad, -(-(slots_total - least) // window))))
    load = [0] * nrad
    shift = [0] * groups
    for s in sorted(range(groups), key=lambda s: nwin[s]):
        best = None
        for sh in range(nrad):
            trial = load[:]
            for w in range(nwin[s], nrad):
                trial[(w + sh) % nrad] += 1
            key = (max(trial), sum(x * x for x in trial))
            if best is None or key < best[0]:
                best = (key, sh, trial)
        shift[s], load = best[1], best[2]
    lists = []
    for r in range(nrad):
        lists.append([s for s in range(groups) if (r - shift[s]) % nrad < nwin[s]])
    count = max(len(x) for x in lists)
    pos_tab, win_tab, ok_tab = [], [], []
    for r in range(nrad):
        entries = lists[r] + [lists[r][0]] * (count - len(lists[r]))
        pos_tab.append(entries)
        win_tab.append([(r - shift[s]) % nrad for s in entries])
        ok_tab.append([1] * len(lists[r]) + [0] * (count - len(lists[r])))
    src_r, src_j, src_ok = [], [], []
    for s in range(groups):
        for w in range(nrad):
            r = (w + shift[s]) % nrad
            live = w < nwin[s]
            src_r.append(r)
            src_j.append(lists[r].index(s) if live else 0)
            src_ok.append(1 if live else 0)
    dest_tab = [[(w + shift[s]) % nrad for w in range(nrad)] for s in range(groups)]
    return dict(count=count, pos=pos_tab, win=win_tab, ok=ok_tab, src_r=src_r, src_j=src_j,
                src_ok=src_ok, dest=dest_tab)


def pack_kernel(picks_ref, dest_ref, *refs):
    x_refs, o_ref = refs[:-1], refs[-1]
    nrad, window = o_ref.shape[0] // len(x_refs), o_ref.shape[-1]
    for i, x_ref in enumerate(x_refs):
        for w in range(nrad):
            o_ref[i * nrad + dest_ref[w]] = x_ref[:, 0:1, :, w * window:(w + 1) * window]


def pack(spectra, picks, dests, groups, nrad, per_group, step=4):
    comps, rows_here, shells_here, slots_total = spectra.shape
    window = slots_total // nrad
    picks_total = groups * per_group

    def in_map(i):
        return lambda q, p, d: (0, p[q * step + i], 0, 0)

    def out_map(q, p, d):
        return (q, 0, 0, 0, 0)

    assert per_group == 1 and picks_total % step == 0
    return pl.pallas_call(
        pack_kernel,
        out_shape=jax.ShapeDtypeStruct(
            (groups * nrad, comps, per_group, shells_here, window), spectra.dtype
        ),
        grid_spec=pltpu.PrefetchScalarGridSpec(
            num_scalar_prefetch=2,
            grid=(picks_total // step,),
            in_specs=[
                pl.BlockSpec((comps, 1, shells_here, slots_total), in_map(i))
                for i in range(step)
            ],
            out_specs=pl.BlockSpec((step * nrad, comps, per_group, shells_here, window), out_map),
        ),
    )(picks, dests, *([spectra] * step))


def solve_kernel(pos_ref, x_ref, info_ref, kappa_ref, invden_ref, eig_ref, d_ref, b_ref, o_ref,
                 pad_ref):
    nrad, comps = x_ref.shape[1], x_ref.shape[2]
    sh, window = x_ref.shape[4], x_ref.shape[5]
    nr = nrad * sh
    cols = [x_ref[0, :, c, 0].reshape(nr, window) for c in range(comps)]
    f = jnp.concatenate(cols, axis=1).astype(jnp.float32)
    width = f.shape[1]
    pad_ref[0:PAD, :] = jnp.zeros((PAD, width), jnp.float32)
    pad_ref[PAD + nr:PAD + nr + PAD, :] = jnp.zeros((PAD, width), jnp.float32)
    pad_ref[PAD:PAD + nr, :] = f
    m2 = pad_ref[PAD - 2:PAD - 2 + nr, :]
    m1 = pad_ref[PAD - 1:PAD - 1 + nr, :]
    p1 = pad_ref[PAD + 1:PAD + 1 + nr, :]
    p2 = pad_ref[PAD + 2:PAD + 2 + nr, :]
    second = (-m2 + 16.0 * m1 - 30.0 * f + 16.0 * p1 - p2) / 12.0
    deg = jnp.concatenate([info_ref[0, 0:1, :]] * comps, axis=1)
    live = jnp.concatenate([info_ref[0, 1:2, :]] * comps, axis=1) > 0.5
    lterm = deg * (deg + 1.0)
    damping = lterm * invden_ref[...]
    updated = f + 0.5 * kappa_ref[...] * (second - damping * f)
    updated = jnp.where(live, updated, 0.0).astype(jnp.bfloat16)
    projected = jnp.dot(d_ref[...], updated, preferred_element_type=jnp.float32)
    divisor = eig_ref[...] + 0.5 * lterm / float(nr * nr)
    scaled = (projected / divisor).astype(jnp.bfloat16)
    restored = jnp.dot(b_ref[...], scaled, preferred_element_type=jnp.float32)
    solved = jnp.where(live, restored, 0.0).astype(jnp.bfloat16)
    for c in range(comps):
        o_ref[:, c, 0] = solved[:, c * window:(c + 1) * window].reshape(nrad, sh, window)


def solve(recv, pos, info, kappa, invden, eig, dual_full, basis_full, groups, nrad, per_group):
    _, comps, _, sh, window = recv.shape
    nr = nrad * sh
    count = pos.shape[0]
    assert per_group == 1
    x = recv.reshape(groups, nrad, comps, per_group, sh, window)
    flops = 2 * 2 * nr * nr * window * comps * count
    return pl.pallas_call(
        solve_kernel,
        out_shape=jax.ShapeDtypeStruct((nrad, comps, count, sh, window), jnp.bfloat16),
        grid_spec=pltpu.PrefetchScalarGridSpec(
            num_scalar_prefetch=1,
            grid=(count,),
            in_specs=[
                pl.BlockSpec((1, nrad, comps, 1, sh, window), lambda q, p: (p[q], 0, 0, 0, 0, 0)),
                pl.BlockSpec((1, 8, window), lambda q, p: (q, 0, 0)),
                pl.BlockSpec((nr, 1), lambda q, p: (0, 0)),
                pl.BlockSpec((nr, 1), lambda q, p: (0, 0)),
                pl.BlockSpec((nr, 1), lambda q, p: (0, 0)),
                pl.BlockSpec((nr, nr), lambda q, p: (0, 0)),
                pl.BlockSpec((nr, nr), lambda q, p: (0, 0)),
            ],
            out_specs=pl.BlockSpec((nrad, comps, 1, sh, window), lambda q, p: (0, 0, q, 0, 0)),
            scratch_shapes=[pltpu.VMEM((nr + 2 * PAD, comps * window), jnp.float32)],
        ),
        compiler_params=pltpu.CompilerParams(vmem_limit_bytes=48 * 1024 * 1024),
        cost_estimate=pl.CostEstimate(
            flops=flops, transcendentals=0,
            bytes_accessed=4 * count * comps * nr * window + 4 * nr * nr,
        ),
    )(pos, x, info, kappa, invden, eig, dual_full, basis_full)


def unpack_kernel(first, r_ref, j_ref, ok_ref, *refs):
    o_ref = refs[-1]
    x_refs = [r for r in refs[:-1] if len(r.shape) == 5]
    nrad, comps, window = x_refs[0].shape[0], x_refs[0].shape[1], x_refs[0].shape[-1]
    split = x_refs[0].shape[2]
    step = o_ref.shape[1]
    s = pl.program_id(0)
    for i in range(step):
        for w in range(nrad):
            k = (first + s * step + i) * nrad + w
            r, j, ok = r_ref[k], j_ref[k], ok_ref[k]
            for c in range(comps):
                if len(x_refs) == 1:
                    blk = x_ref_pick(x_refs[0], r, c, jnp.minimum(j, split - 1))
                else:
                    low = x_ref_pick(x_refs[0], r, c, jnp.minimum(j, split - 1))
                    high = x_ref_pick(x_refs[1], r, c, jnp.maximum(j - split, 0))
                    blk = jnp.where(j < split, low, high)
                o_ref[c, i, :, w * window:(w + 1) * window] = jnp.where(
                    ok > 0, blk, jnp.zeros_like(blk)
                )


def x_ref_pick(x_ref, r, c, j):
    return x_ref[r, c, j]


def unpack(gots, first, last, prev, src_r, src_j, src_ok, rows_here, step=4):
    nrad, comps, _, sh, window = gots[0].shape
    shape = (comps, rows_here, sh, nrad * window)
    assert first % step == 0 and last % step == 0
    in_specs = [
        pl.BlockSpec(g.shape, lambda s, a, b, c: (0, 0, 0, 0, 0)) for g in gots
    ]
    args = list(gots)
    aliases = {}
    if prev is not None:
        in_specs.append(pl.BlockSpec(memory_space=pl.ANY))
        args.append(prev)
        aliases = {3 + len(gots): 0}
    base = first // step
    return pl.pallas_call(
        functools.partial(unpack_kernel, first),
        out_shape=jax.ShapeDtypeStruct(shape, gots[0].dtype),
        grid_spec=pltpu.PrefetchScalarGridSpec(
            num_scalar_prefetch=3,
            grid=((last - first) // step,),
            in_specs=in_specs,
            out_specs=pl.BlockSpec(
                (comps, step, sh, nrad * window), lambda s, a, b, c: (0, base + s, 0, 0)
            ),
        ),
        input_output_aliases=aliases,
        compiler_params=pltpu.CompilerParams(vmem_limit_bytes=48 * 1024 * 1024),
    )(src_r, src_j, src_ok, *args)


def on_device(
    spectra, diffusivity, eigenvalues, radial_basis, dual_basis, degree_count, order_slot
):
    comps, rows_here, shells_here, slots_total = spectra.shape
    shells_total = diffusivity.shape[0]
    orders_total = degree_count.shape[0]
    groups = lax.axis_size("mode")
    nrad = lax.axis_size("rad")
    per_group = rows_here // groups
    window = slots_total // nrad
    me_mode = lax.axis_index("mode")
    me_rad = lax.axis_index("rad")
    tab = layout_tables(groups, nrad, rows_here, slots_total, orders_total)

    picks = (
        lax.dynamic_slice_in_dim(
            order_slot.reshape(groups, groups, per_group), me_mode, 1, 1
        ).reshape(groups * per_group)
        - me_mode * rows_here
    )
    dests = jnp.asarray(tab["dest"], jnp.int32)[me_mode]
    send = pack(spectra, picks, dests, groups, nrad, per_group)
    recv = lax.all_to_all(send, ("mode", "rad"), 0, 0, tiled=True)

    pos = jnp.asarray(tab["pos"], jnp.int32)[me_rad]
    win = jnp.asarray(tab["win"], jnp.int32)[me_rad]
    ok = jnp.asarray(tab["ok"], jnp.int32)[me_rad]
    in_rows = jnp.take(order_slot, me_mode * rows_here + pos)
    orders = in_rows * slots_total // (2 * orders_total)
    slot_ids = win[:, None] * window + jnp.arange(window, dtype=jnp.int32)[None, :]
    degree = (orders[:, None] + slot_ids).astype(jnp.float32)
    live = (slot_ids < jnp.take(degree_count, in_rows)[:, None]) & (ok[:, None] > 0)
    count = tab["count"]
    info = jnp.zeros((count, 8, window), jnp.float32)
    info = info.at[:, 0, :].set(degree)
    info = info.at[:, 1, :].set(live.astype(jnp.float32))

    radius = 1.2 + jnp.arange(shells_total, dtype=jnp.int32).astype(jnp.float32) / shells_total
    invden = (1.0 / ((shells_total * radius) ** 2)).reshape(shells_total, 1)
    kappa = diffusivity.reshape(shells_total, 1)
    eig = eigenvalues.reshape(shells_total, 1)

    identity = jnp.eye(shells_total, dtype=jnp.float32)
    basis_full = (identity + radial_basis.astype(jnp.float32)).astype(jnp.bfloat16)
    dual_full = (identity + dual_basis.astype(jnp.float32)).astype(jnp.bfloat16)
    split = SPLIT
    gots = []
    for lo, hi in ((0, split), (split, count)):
        back = solve(recv, pos[lo:hi], info[lo:hi], kappa, invden, eig, dual_full, basis_full,
                     groups, nrad, per_group)
        gots.append(lax.all_to_all(back, "rad", 0, 0, tiled=True))
    src_r = jnp.asarray(tab["src_r"], jnp.int32)
    src_j = jnp.asarray(tab["src_j"], jnp.int32)
    src_ok = jnp.asarray(tab["src_ok"], jnp.int32)
    out = unpack(gots[:1], 0, split, None, src_r, src_j, src_ok, rows_here)
    return unpack(gots, split, rows_here, out, src_r, src_j, src_ok, rows_here)


def solution(mesh):
    placed = (P(None, "mode", "rad", None), P(), P(), P(), P(), P(), P())
    return jax.shard_map(
        on_device,
        mesh=mesh,
        in_specs=placed,
        out_specs=P(None, "mode", "rad", None),
        check_vma=False,
    )
```

```python
import functools

import jax
import numpy as np
import jax.numpy as jnp
from jax import lax
from jax.experimental import pallas as pl
from jax.experimental.pallas import tpu as pltpu
from jax.sharding import PartitionSpec as P

PAD = 8


def layout_tables(groups, nrad, rows_here, slots_total, orders_total):
    window = slots_total // nrad
    nwin = []
    for s in range(groups):
        least = (s * rows_here) * slots_total // (2 * orders_total)
        nwin.append(max(1, min(nrad, -(-(slots_total - least) // window))))
    load = [0] * nrad
    shift = [0] * groups
    for s in sorted(range(groups), key=lambda s: nwin[s]):
        best = None
        for sh in range(nrad):
            trial = load[:]
            for w in range(nwin[s], nrad):
                trial[(w + sh) % nrad] += 1
            key = (max(trial), sum(x * x for x in trial))
            if best is None or key < best[0]:
                best = (key, sh, trial)
        shift[s], load = best[1], best[2]
    lists = []
    for r in range(nrad):
        lists.append([s for s in range(groups) if (r - shift[s]) % nrad < nwin[s]])
    count = max(len(x) for x in lists)
    pos_tab, win_tab, ok_tab = [], [], []
    for r in range(nrad):
        entries = lists[r] + [lists[r][0]] * (count - len(lists[r]))
        pos_tab.append(entries)
        win_tab.append([(r - shift[s]) % nrad for s in entries])
        ok_tab.append([1] * len(lists[r]) + [0] * (count - len(lists[r])))
    src_r, src_j, src_ok = [], [], []
    for s in range(groups):
        for w in range(nrad):
            r = (w + shift[s]) % nrad
            live = w < nwin[s]
            src_r.append(r)
            src_j.append(lists[r].index(s) if live else 0)
            src_ok.append(1 if live else 0)
    dest_tab = [[(w + shift[s]) % nrad for w in range(nrad)] for s in range(groups)]
    return dict(count=count, pos=pos_tab, win=win_tab, ok=ok_tab, src_r=src_r, src_j=src_j,
                src_ok=src_ok, dest=dest_tab)


def pack_kernel(picks_total, prefetch_ref, *refs):
    x_refs, o_ref = refs[:-1], refs[-1]
    nrad, window = o_ref.shape[0] // len(x_refs), o_ref.shape[-1]
    for i, x_ref in enumerate(x_refs):
        for w in range(nrad):
            dest = prefetch_ref[picks_total + w]
            o_ref[i * nrad + dest] = x_ref[:, 0:1, :, w * window:(w + 1) * window]


def pack(spectra, prefetch, comp, groups, nrad, per_group, step=4):
    comps, rows_here, shells_here, slots_total = spectra.shape
    window = slots_total // nrad
    picks_total = groups * per_group

    def in_map(i):
        return lambda q, p: (comp, p[q * step + i], 0, 0)

    def out_map(q, p):
        return (q, 0, 0, 0, 0)

    assert per_group == 1 and picks_total % step == 0
    return pl.pallas_call(
        functools.partial(pack_kernel, picks_total),
        out_shape=jax.ShapeDtypeStruct(
            (groups * nrad, 1, per_group, shells_here, window), spectra.dtype
        ),
        grid_spec=pltpu.PrefetchScalarGridSpec(
            num_scalar_prefetch=1,
            grid=(picks_total // step,),
            in_specs=[
                pl.BlockSpec((1, 1, shells_here, slots_total), in_map(i))
                for i in range(step)
            ],
            out_specs=pl.BlockSpec((step * nrad, 1, per_group, shells_here, window), out_map),
        ),
    )(prefetch, *([spectra] * step))


def solve_kernel(pos_ref, *refs):
    npos = len(refs) - 8
    x_refs = refs[:npos]
    info_ref, kappa_ref, invden_ref, eig_ref, d_ref, b_ref, o_ref, pad_ref = refs[npos:]
    nrad = x_refs[0].shape[1]
    sh, window = x_refs[0].shape[4], x_refs[0].shape[5]
    nr = nrad * sh
    cols = [x_ref[0, :, 0, 0].reshape(nr, window) for x_ref in x_refs]
    f = jnp.concatenate(cols, axis=1).astype(jnp.float32)
    width = f.shape[1]
    pad_ref[0:PAD, :] = jnp.zeros((PAD, width), jnp.float32)
    pad_ref[PAD + nr:PAD + nr + PAD, :] = jnp.zeros((PAD, width), jnp.float32)
    pad_ref[PAD:PAD + nr, :] = f
    m2 = pad_ref[PAD - 2:PAD - 2 + nr, :]
    m1 = pad_ref[PAD - 1:PAD - 1 + nr, :]
    p1 = pad_ref[PAD + 1:PAD + 1 + nr, :]
    p2 = pad_ref[PAD + 2:PAD + 2 + nr, :]
    second = (-m2 + 16.0 * m1 - 30.0 * f + 16.0 * p1 - p2) / 12.0
    deg = jnp.concatenate([info_ref[j, 0:1, :] for j in range(npos)], axis=1)
    live = jnp.concatenate([info_ref[j, 1:2, :] for j in range(npos)], axis=1) > 0.5
    lterm = deg * (deg + 1.0)
    damping = lterm * invden_ref[...]
    updated = f + 0.5 * kappa_ref[...] * (second - damping * f)
    updated = jnp.where(live, updated, 0.0).astype(jnp.bfloat16)
    projected = jnp.dot(d_ref[...], updated, preferred_element_type=jnp.float32)
    divisor = eig_ref[...] + 0.5 * lterm / float(nr * nr)
    scaled = (projected / divisor).astype(jnp.bfloat16)
    restored = jnp.dot(b_ref[...], scaled, preferred_element_type=jnp.float32)
    solved = jnp.where(live, restored, 0.0).astype(jnp.bfloat16)
    for j in range(npos):
        o_ref[:, 0, j] = solved[:, j * window:(j + 1) * window].reshape(nrad, sh, window)


def solve(recv, pos, info, kappa, invden, eig, dual_full, basis_full, groups, nrad, per_group,
          npos=1):
    _, _, _, sh, window = recv.shape
    nr = nrad * sh
    count = pos.shape[0]
    assert per_group == 1 and count % npos == 0
    x = recv.reshape(groups, nrad, 1, per_group, sh, window)
    flops = 2 * 2 * nr * nr * window * count

    def x_map(j):
        return lambda q, p: (p[q * npos + j], 0, 0, 0, 0, 0)

    return pl.pallas_call(
        solve_kernel,
        out_shape=jax.ShapeDtypeStruct((nrad, 1, count, sh, window), jnp.bfloat16),
        grid_spec=pltpu.PrefetchScalarGridSpec(
            num_scalar_prefetch=1,
            grid=(count // npos,),
            in_specs=[
                pl.BlockSpec((1, nrad, 1, 1, sh, window), x_map(j)) for j in range(npos)
            ] + [
                pl.BlockSpec((npos, 8, window), lambda q, p: (q, 0, 0)),
                pl.BlockSpec((nr, 1), lambda q, p: (0, 0)),
                pl.BlockSpec((nr, 1), lambda q, p: (0, 0)),
                pl.BlockSpec((nr, 1), lambda q, p: (0, 0)),
                pl.BlockSpec((nr, nr), lambda q, p: (0, 0)),
                pl.BlockSpec((nr, nr), lambda q, p: (0, 0)),
            ],
            out_specs=pl.BlockSpec((nrad, 1, npos, sh, window), lambda q, p: (0, 0, q, 0, 0)),
            scratch_shapes=[pltpu.VMEM((nr + 2 * PAD, npos * window), jnp.float32)],
        ),
        compiler_params=pltpu.CompilerParams(vmem_limit_bytes=48 * 1024 * 1024),
        cost_estimate=pl.CostEstimate(
            flops=flops, transcendentals=0, bytes_accessed=4 * count * nr * window + 4 * nr * nr
        ),
    )(pos, *([x] * npos), info, kappa, invden, eig, dual_full, basis_full)


def unpack_kernel(r_ref, j_ref, ok_ref, x_ref, *refs):
    o_ref = refs[-1]
    nrad, window = x_ref.shape[0], x_ref.shape[-1]
    step = o_ref.shape[1]
    s = pl.program_id(0)
    for i in range(step):
        for w in range(nrad):
            k = (s * step + i) * nrad + w
            blk = x_ref[r_ref[k], 0, j_ref[k]]
            o_ref[0, i, :, w * window:(w + 1) * window] = jnp.where(
                ok_ref[k] > 0, blk, jnp.zeros_like(blk)
            )


def unpack(got, comp, comps, prev, src_r, src_j, src_ok, rows_here, step=4):
    nrad, _, count, sh, window = got.shape
    shape = (comps, rows_here, sh, nrad * window)
    in_specs = [pl.BlockSpec((nrad, 1, count, sh, window), lambda s, a, b, c: (0, 0, 0, 0, 0))]
    args = [got]
    aliases = {}
    if prev is not None:
        in_specs.append(pl.BlockSpec(memory_space=pl.ANY))
        args.append(prev)
        aliases = {4: 0}
    return pl.pallas_call(
        unpack_kernel,
        out_shape=jax.ShapeDtypeStruct(shape, got.dtype),
        grid_spec=pltpu.PrefetchScalarGridSpec(
            num_scalar_prefetch=3,
            grid=(rows_here // step,),
            in_specs=in_specs,
            out_specs=pl.BlockSpec(
                (1, step, sh, nrad * window), lambda s, a, b, c: (comp, s, 0, 0)
            ),
        ),
        input_output_aliases=aliases,
        compiler_params=pltpu.CompilerParams(vmem_limit_bytes=48 * 1024 * 1024),
    )(src_r, src_j, src_ok, *args)


def on_device(
    spectra, diffusivity, eigenvalues, radial_basis, dual_basis, degree_count, order_slot
):
    comps, rows_here, shells_here, slots_total = spectra.shape
    shells_total = diffusivity.shape[0]
    orders_total = degree_count.shape[0]
    groups = lax.axis_size("mode")
    nrad = lax.axis_size("rad")
    per_group = rows_here // groups
    window = slots_total // nrad
    me_mode = lax.axis_index("mode")
    me_rad = lax.axis_index("rad")
    tab = layout_tables(groups, nrad, rows_here, slots_total, orders_total)

    slots = np.arange(groups * per_group)
    where = (slots // per_group) * rows_here + slots % per_group
    table = np.concatenate(
        [np.zeros((groups, groups * per_group), np.int64), np.asarray(tab["dest"])], axis=1
    )
    index = np.concatenate([where, np.zeros(nrad, np.int64)]).astype(np.int32)
    is_pick = np.concatenate([np.ones(groups * per_group), np.zeros(nrad)]).astype(np.int32)
    looked = jnp.take(order_slot, jnp.asarray(index) + me_mode * per_group)
    prefetch = jnp.where(
        jnp.asarray(is_pick) > 0,
        looked - me_mode * rows_here,
        jnp.take(jnp.asarray(table.reshape(-1), jnp.int32),
                 me_mode * table.shape[1] + jnp.arange(table.shape[1], dtype=jnp.int32)),
    )
    recvs = []
    for comp in range(comps):
        send = pack(spectra, prefetch, comp, groups, nrad, per_group)
        recvs.append(lax.all_to_all(send, ("mode", "rad"), 0, 0, tiled=True))

    pos = jnp.asarray(tab["pos"], jnp.int32)[me_rad]
    win = jnp.asarray(tab["win"], jnp.int32)[me_rad]
    ok = jnp.asarray(tab["ok"], jnp.int32)[me_rad]
    in_rows = jnp.take(order_slot, me_mode * rows_here + pos)
    orders = in_rows * slots_total // (2 * orders_total)
    slot_ids = win[:, None] * window + jnp.arange(window, dtype=jnp.int32)[None, :]
    degree = (orders[:, None] + slot_ids).astype(jnp.float32)
    live = (slot_ids < jnp.take(degree_count, in_rows)[:, None]) & (ok[:, None] > 0)
    count = tab["count"]
    info = jnp.zeros((count, 8, window), jnp.float32)
    info = info.at[:, 0, :].set(degree)
    info = info.at[:, 1, :].set(live.astype(jnp.float32))

    radius = 1.2 + jnp.arange(shells_total, dtype=jnp.int32).astype(jnp.float32) / shells_total
    invden = (1.0 / ((shells_total * radius) ** 2)).reshape(shells_total, 1)
    kappa = diffusivity.reshape(shells_total, 1)
    eig = eigenvalues.reshape(shells_total, 1)

    identity = jnp.eye(shells_total, dtype=jnp.float32)
    basis_full = (identity + radial_basis.astype(jnp.float32)).astype(jnp.bfloat16)
    dual_full = (identity + dual_basis.astype(jnp.float32)).astype(jnp.bfloat16)
    gots = []
    for recv in recvs:
        back = solve(recv, pos, info, kappa, invden, eig, dual_full, basis_full, groups, nrad,
                     per_group)
        gots.append(lax.all_to_all(back, "rad", 0, 0, tiled=True))
    src_r = jnp.asarray(tab["src_r"], jnp.int32)
    src_j = jnp.asarray(tab["src_j"], jnp.int32)
    src_ok = jnp.asarray(tab["src_ok"], jnp.int32)
    out = None
    for comp, got in enumerate(gots):
        out = unpack(got, comp, comps, out, src_r, src_j, src_ok, rows_here)
    return out


def solution(mesh):
    placed = (P(None, "mode", "rad", None), P(), P(), P(), P(), P(), P())
    return jax.shard_map(
        on_device,
        mesh=mesh,
        in_specs=placed,
        out_specs=P(None, "mode", "rad", None),
        check_vma=False,
    )
```

```python
import functools

import jax
import jax.numpy as jnp
from jax import lax
from jax.experimental import pallas as pl
from jax.experimental.pallas import tpu as pltpu
from jax.sharding import PartitionSpec as P

PAD = 8


def layout_tables(groups, nrad, rows_here, slots_total, orders_total):
    window = slots_total // nrad
    nwin = []
    for s in range(groups):
        least = (s * rows_here) * slots_total // (2 * orders_total)
        nwin.append(max(1, min(nrad, -(-(slots_total - least) // window))))
    load = [0] * nrad
    shift = [0] * groups
    for s in sorted(range(groups), key=lambda s: nwin[s]):
        best = None
        for sh in range(nrad):
            trial = load[:]
            for w in range(nwin[s], nrad):
                trial[(w + sh) % nrad] += 1
            key = (max(trial), sum(x * x for x in trial))
            if best is None or key < best[0]:
                best = (key, sh, trial)
        shift[s], load = best[1], best[2]
    lists = []
    for r in range(nrad):
        lists.append([s for s in range(groups) if (r - shift[s]) % nrad < nwin[s]])
    count = max(len(x) for x in lists)
    pos_tab, win_tab, ok_tab = [], [], []
    for r in range(nrad):
        entries = lists[r] + [lists[r][0]] * (count - len(lists[r]))
        pos_tab.append(entries)
        win_tab.append([(r - shift[s]) % nrad for s in entries])
        ok_tab.append([1] * len(lists[r]) + [0] * (count - len(lists[r])))
    src_r, src_j, src_ok = [], [], []
    for s in range(groups):
        for w in range(nrad):
            r = (w + shift[s]) % nrad
            live = w < nwin[s]
            src_r.append(r)
            src_j.append(lists[r].index(s) if live else 0)
            src_ok.append(1 if live else 0)
    dest_tab = [[(w + shift[s]) % nrad for w in range(nrad)] for s in range(groups)]
    return dict(count=count, pos=pos_tab, win=win_tab, ok=ok_tab, src_r=src_r, src_j=src_j,
                src_ok=src_ok, dest=dest_tab)


def pack_kernel(order_ref, shift_ref, *refs):
    x_refs, o_ref = refs[:-1], refs[-1]
    nrad, window = o_ref.shape[0] // len(x_refs), o_ref.shape[-1]
    turn = shift_ref[lax.axis_index("mode")]
    for i, x_ref in enumerate(x_refs):
        for w in range(nrad):
            o_ref[i * nrad + (w + turn) % nrad] = x_ref[:, 0:1, :, w * window:(w + 1) * window]


def pack(spectra, order_slot, shifts, comp, groups, nrad, per_group, step=4):
    comps, rows_here, shells_here, slots_total = spectra.shape
    window = slots_total // nrad
    picks_total = groups * per_group

    def in_map(i):
        def index(q, p, d):
            me = lax.axis_index("mode")
            return (comp, p[(q * step + i) * rows_here + me * per_group] - me * rows_here, 0, 0)

        return index

    def out_map(q, p, d):
        return (q, 0, 0, 0, 0)

    assert per_group == 1 and picks_total % step == 0
    return pl.pallas_call(
        pack_kernel,
        out_shape=jax.ShapeDtypeStruct(
            (groups * nrad, 1, per_group, shells_here, window), spectra.dtype
        ),
        grid_spec=pltpu.PrefetchScalarGridSpec(
            num_scalar_prefetch=2,
            grid=(picks_total // step,),
            in_specs=[
                pl.BlockSpec((1, 1, shells_here, slots_total), in_map(i))
                for i in range(step)
            ],
            out_specs=pl.BlockSpec((step * nrad, 1, per_group, shells_here, window), out_map),
        ),
    )(order_slot, shifts, *([spectra] * step))


def solve_kernel(pos_ref, *refs):
    npos = len(refs) - 8
    x_refs = refs[:npos]
    info_ref, kappa_ref, invden_ref, eig_ref, d_ref, b_ref, o_ref, pad_ref = refs[npos:]
    nrad = x_refs[0].shape[1]
    sh, window = x_refs[0].shape[4], x_refs[0].shape[5]
    nr = nrad * sh
    cols = [x_ref[0, :, 0, 0].reshape(nr, window) for x_ref in x_refs]
    f = jnp.concatenate(cols, axis=1).astype(jnp.float32)
    width = f.shape[1]
    pad_ref[0:PAD, :] = jnp.zeros((PAD, width), jnp.float32)
    pad_ref[PAD + nr:PAD + nr + PAD, :] = jnp.zeros((PAD, width), jnp.float32)
    pad_ref[PAD:PAD + nr, :] = f
    m2 = pad_ref[PAD - 2:PAD - 2 + nr, :]
    m1 = pad_ref[PAD - 1:PAD - 1 + nr, :]
    p1 = pad_ref[PAD + 1:PAD + 1 + nr, :]
    p2 = pad_ref[PAD + 2:PAD + 2 + nr, :]
    second = (-m2 + 16.0 * m1 - 30.0 * f + 16.0 * p1 - p2) / 12.0
    deg = jnp.concatenate([info_ref[j, 0:1, :] for j in range(npos)], axis=1)
    live = jnp.concatenate([info_ref[j, 1:2, :] for j in range(npos)], axis=1) > 0.5
    lterm = deg * (deg + 1.0)
    damping = lterm * invden_ref[...]
    updated = f + 0.5 * kappa_ref[...] * (second - damping * f)
    updated = jnp.where(live, updated, 0.0).astype(jnp.bfloat16)
    projected = jnp.dot(d_ref[...], updated, preferred_element_type=jnp.float32)
    divisor = eig_ref[...] + 0.5 * lterm / float(nr * nr)
    scaled = (projected / divisor).astype(jnp.bfloat16)
    restored = jnp.dot(b_ref[...], scaled, preferred_element_type=jnp.float32)
    solved = jnp.where(live, restored, 0.0).astype(jnp.bfloat16)
    for j in range(npos):
        o_ref[:, 0, j] = solved[:, j * window:(j + 1) * window].reshape(nrad, sh, window)


def solve(recv, pos, info, kappa, invden, eig, dual_full, basis_full, groups, nrad, per_group,
          npos=1):
    _, _, _, sh, window = recv.shape
    nr = nrad * sh
    count = pos.shape[0]
    assert per_group == 1 and count % npos == 0
    x = recv.reshape(groups, nrad, 1, per_group, sh, window)
    flops = 2 * 2 * nr * nr * window * count

    def x_map(j):
        return lambda q, p: (p[q * npos + j], 0, 0, 0, 0, 0)

    return pl.pallas_call(
        solve_kernel,
        out_shape=jax.ShapeDtypeStruct((nrad, 1, count, sh, window), jnp.bfloat16),
        grid_spec=pltpu.PrefetchScalarGridSpec(
            num_scalar_prefetch=1,
            grid=(count // npos,),
            in_specs=[
                pl.BlockSpec((1, nrad, 1, 1, sh, window), x_map(j)) for j in range(npos)
            ] + [
                pl.BlockSpec((npos, 8, window), lambda q, p: (q, 0, 0)),
                pl.BlockSpec((nr, 1), lambda q, p: (0, 0)),
                pl.BlockSpec((nr, 1), lambda q, p: (0, 0)),
                pl.BlockSpec((nr, 1), lambda q, p: (0, 0)),
                pl.BlockSpec((nr, nr), lambda q, p: (0, 0)),
                pl.BlockSpec((nr, nr), lambda q, p: (0, 0)),
            ],
            out_specs=pl.BlockSpec((nrad, 1, npos, sh, window), lambda q, p: (0, 0, q, 0, 0)),
            scratch_shapes=[pltpu.VMEM((nr + 2 * PAD, npos * window), jnp.float32)],
        ),
        compiler_params=pltpu.CompilerParams(vmem_limit_bytes=48 * 1024 * 1024),
        cost_estimate=pl.CostEstimate(
            flops=flops, transcendentals=0, bytes_accessed=4 * count * nr * window + 4 * nr * nr
        ),
    )(pos, *([x] * npos), info, kappa, invden, eig, dual_full, basis_full)


def unpack_kernel(r_ref, j_ref, ok_ref, x_ref, *refs):
    o_ref = refs[-1]
    nrad, window = x_ref.shape[0], x_ref.shape[-1]
    step = o_ref.shape[1]
    s = pl.program_id(0)
    for i in range(step):
        for w in range(nrad):
            k = (s * step + i) * nrad + w
            blk = x_ref[r_ref[k], 0, j_ref[k]]
            o_ref[0, i, :, w * window:(w + 1) * window] = jnp.where(
                ok_ref[k] > 0, blk, jnp.zeros_like(blk)
            )


def unpack(got, comp, comps, prev, src_r, src_j, src_ok, rows_here, step=4):
    nrad, _, count, sh, window = got.shape
    shape = (comps, rows_here, sh, nrad * window)
    in_specs = [pl.BlockSpec((nrad, 1, count, sh, window), lambda s, a, b, c: (0, 0, 0, 0, 0))]
    args = [got]
    aliases = {}
    if prev is not None:
        in_specs.append(pl.BlockSpec(memory_space=pl.ANY))
        args.append(prev)
        aliases = {4: 0}
    return pl.pallas_call(
        unpack_kernel,
        out_shape=jax.ShapeDtypeStruct(shape, got.dtype),
        grid_spec=pltpu.PrefetchScalarGridSpec(
            num_scalar_prefetch=3,
            grid=(rows_here // step,),
            in_specs=in_specs,
            out_specs=pl.BlockSpec(
                (1, step, sh, nrad * window), lambda s, a, b, c: (comp, s, 0, 0)
            ),
        ),
        input_output_aliases=aliases,
        compiler_params=pltpu.CompilerParams(vmem_limit_bytes=48 * 1024 * 1024),
    )(src_r, src_j, src_ok, *args)


def on_device(
    spectra, diffusivity, eigenvalues, radial_basis, dual_basis, degree_count, order_slot
):
    comps, rows_here, shells_here, slots_total = spectra.shape
    shells_total = diffusivity.shape[0]
    orders_total = degree_count.shape[0]
    groups = lax.axis_size("mode")
    nrad = lax.axis_size("rad")
    per_group = rows_here // groups
    window = slots_total // nrad
    me_mode = lax.axis_index("mode")
    me_rad = lax.axis_index("rad")
    tab = layout_tables(groups, nrad, rows_here, slots_total, orders_total)

    shifts = jnp.asarray([row[0] for row in tab["dest"]], jnp.int32)
    recvs = []
    for comp in range(comps):
        send = pack(spectra, order_slot, shifts, comp, groups, nrad, per_group)
        recvs.append(lax.all_to_all(send, ("mode", "rad"), 0, 0, tiled=True))

    pos = jnp.asarray(tab["pos"], jnp.int32)[me_rad]
    win = jnp.asarray(tab["win"], jnp.int32)[me_rad]
    ok = jnp.asarray(tab["ok"], jnp.int32)[me_rad]
    in_rows = jnp.take(order_slot, me_mode * rows_here + pos)
    orders = in_rows * slots_total // (2 * orders_total)
    slot_ids = win[:, None] * window + jnp.arange(window, dtype=jnp.int32)[None, :]
    degree = (orders[:, None] + slot_ids).astype(jnp.float32)
    live = (slot_ids < jnp.take(degree_count, in_rows)[:, None]) & (ok[:, None] > 0)
    count = tab["count"]
    info = jnp.zeros((count, 8, window), jnp.float32)
    info = info.at[:, 0, :].set(degree)
    info = info.at[:, 1, :].set(live.astype(jnp.float32))

    radius = 1.2 + jnp.arange(shells_total, dtype=jnp.int32).astype(jnp.float32) / shells_total
    invden = (1.0 / ((shells_total * radius) ** 2)).reshape(shells_total, 1)
    kappa = diffusivity.reshape(shells_total, 1)
    eig = eigenvalues.reshape(shells_total, 1)

    identity = jnp.eye(shells_total, dtype=jnp.float32)
    basis_full = (identity + radial_basis.astype(jnp.float32)).astype(jnp.bfloat16)
    dual_full = (identity + dual_basis.astype(jnp.float32)).astype(jnp.bfloat16)
    gots = []
    for recv in recvs:
        back = solve(recv, pos, info, kappa, invden, eig, dual_full, basis_full, groups, nrad,
                     per_group)
        gots.append(lax.all_to_all(back, "rad", 0, 0, tiled=True))
    src_r = jnp.asarray(tab["src_r"], jnp.int32)
    src_j = jnp.asarray(tab["src_j"], jnp.int32)
    src_ok = jnp.asarray(tab["src_ok"], jnp.int32)
    out = None
    for comp, got in enumerate(gots):
        out = unpack(got, comp, comps, out, src_r, src_j, src_ok, rows_here)
    return out


def solution(mesh):
    placed = (P(None, "mode", "rad", None), P(), P(), P(), P(), P(), P())
    return jax.shard_map(
        on_device,
        mesh=mesh,
        in_specs=placed,
        out_specs=P(None, "mode", "rad", None),
        check_vma=False,
    )
```

```python
import functools

import jax
import jax.numpy as jnp
from jax import lax
from jax.experimental import pallas as pl
from jax.experimental.pallas import tpu as pltpu
from jax.sharding import PartitionSpec as P

PAD = 8


def layout_tables(groups, nrad, rows_here, slots_total, orders_total):
    window = slots_total // nrad
    nwin = []
    for s in range(groups):
        least = (s * rows_here) * slots_total // (2 * orders_total)
        nwin.append(max(1, min(nrad, -(-(slots_total - least) // window))))
    load = [0] * nrad
    shift = [0] * groups
    for s in sorted(range(groups), key=lambda s: nwin[s]):
        best = None
        for sh in range(nrad):
            trial = load[:]
            for w in range(nwin[s], nrad):
                trial[(w + sh) % nrad] += 1
            key = (max(trial), sum(x * x for x in trial))
            if best is None or key < best[0]:
                best = (key, sh, trial)
        shift[s], load = best[1], best[2]
    lists = []
    for r in range(nrad):
        lists.append([s for s in range(groups) if (r - shift[s]) % nrad < nwin[s]])
    count = max(len(x) for x in lists)
    pos_tab, win_tab, ok_tab = [], [], []
    for r in range(nrad):
        entries = lists[r] + [lists[r][0]] * (count - len(lists[r]))
        pos_tab.append(entries)
        win_tab.append([(r - shift[s]) % nrad for s in entries])
        ok_tab.append([1] * len(lists[r]) + [0] * (count - len(lists[r])))
    src_r, src_j, src_ok = [], [], []
    for s in range(groups):
        for w in range(nrad):
            r = (w + shift[s]) % nrad
            live = w < nwin[s]
            src_r.append(r)
            src_j.append(lists[r].index(s) if live else 0)
            src_ok.append(1 if live else 0)
    dest_tab = [[(w + shift[s]) % nrad for w in range(nrad)] for s in range(groups)]
    return dict(count=count, pos=pos_tab, win=win_tab, ok=ok_tab, src_r=src_r, src_j=src_j,
                src_ok=src_ok, dest=dest_tab)


def pack_kernel(order_ref, shift_ref, *refs):
    x_refs, o_ref = refs[:-1], refs[-1]
    nrad, window = o_ref.shape[0] // len(x_refs), o_ref.shape[-1]
    turn = shift_ref[lax.axis_index("mode")]
    for i, x_ref in enumerate(x_refs):
        for w in range(nrad):
            o_ref[i * nrad + (w + turn) % nrad] = x_ref[:, 0:1, :, w * window:(w + 1) * window]


def pack(spectra, order_slot, shifts, comp, groups, nrad, per_group, step=8):
    comps, rows_here, shells_here, slots_total = spectra.shape
    window = slots_total // nrad
    picks_total = groups * per_group

    def in_map(i):
        def index(q, p, d):
            me = lax.axis_index("mode")
            return (comp, p[(q * step + i) * rows_here + me * per_group] - me * rows_here, 0, 0)

        return index

    def out_map(q, p, d):
        return (q, 0, 0, 0, 0)

    assert per_group == 1 and picks_total % step == 0
    return pl.pallas_call(
        pack_kernel,
        out_shape=jax.ShapeDtypeStruct(
            (groups * nrad, 1, per_group, shells_here, window), spectra.dtype
        ),
        grid_spec=pltpu.PrefetchScalarGridSpec(
            num_scalar_prefetch=2,
            grid=(picks_total // step,),
            in_specs=[
                pl.BlockSpec((1, 1, shells_here, slots_total), in_map(i))
                for i in range(step)
            ],
            out_specs=pl.BlockSpec((step * nrad, 1, per_group, shells_here, window), out_map),
        ),
    )(order_slot, shifts, *([spectra] * step))


def solve_kernel(pos_ref, *refs):
    npos = len(refs) - 8
    x_refs = refs[:npos]
    info_ref, kappa_ref, invden_ref, eig_ref, d_ref, b_ref, o_ref, pad_ref = refs[npos:]
    nrad = x_refs[0].shape[1]
    sh, window = x_refs[0].shape[4], x_refs[0].shape[5]
    nr = nrad * sh
    cols = [x_ref[0, :, 0, 0].reshape(nr, window) for x_ref in x_refs]
    f = jnp.concatenate(cols, axis=1).astype(jnp.float32)
    width = f.shape[1]
    pad_ref[0:PAD, :] = jnp.zeros((PAD, width), jnp.float32)
    pad_ref[PAD + nr:PAD + nr + PAD, :] = jnp.zeros((PAD, width), jnp.float32)
    pad_ref[PAD:PAD + nr, :] = f
    m2 = pad_ref[PAD - 2:PAD - 2 + nr, :]
    m1 = pad_ref[PAD - 1:PAD - 1 + nr, :]
    p1 = pad_ref[PAD + 1:PAD + 1 + nr, :]
    p2 = pad_ref[PAD + 2:PAD + 2 + nr, :]
    second = (-m2 + 16.0 * m1 - 30.0 * f + 16.0 * p1 - p2) / 12.0
    deg = jnp.concatenate([info_ref[j, 0:1, :] for j in range(npos)], axis=1)
    live = jnp.concatenate([info_ref[j, 1:2, :] for j in range(npos)], axis=1) > 0.5
    lterm = deg * (deg + 1.0)
    damping = lterm * invden_ref[...]
    updated = f + 0.5 * kappa_ref[...] * (second - damping * f)
    updated = jnp.where(live, updated, 0.0).astype(jnp.bfloat16)
    projected = jnp.dot(d_ref[...], updated, preferred_element_type=jnp.float32)
    divisor = eig_ref[...] + 0.5 * lterm / float(nr * nr)
    scaled = (projected / divisor).astype(jnp.bfloat16)
    restored = jnp.dot(b_ref[...], scaled, preferred_element_type=jnp.float32)
    solved = jnp.where(live, restored, 0.0).astype(jnp.bfloat16)
    for j in range(npos):
        o_ref[:, 0, j] = solved[:, j * window:(j + 1) * window].reshape(nrad, sh, window)


def solve(recv, pos, info, kappa, invden, eig, dual_full, basis_full, groups, nrad, per_group,
          npos=1):
    _, _, _, sh, window = recv.shape
    nr = nrad * sh
    count = pos.shape[0]
    assert per_group == 1 and count % npos == 0
    x = recv.reshape(groups, nrad, 1, per_group, sh, window)
    flops = 2 * 2 * nr * nr * window * count

    def x_map(j):
        return lambda q, p: (p[q * npos + j], 0, 0, 0, 0, 0)

    return pl.pallas_call(
        solve_kernel,
        out_shape=jax.ShapeDtypeStruct((nrad, 1, count, sh, window), jnp.bfloat16),
        grid_spec=pltpu.PrefetchScalarGridSpec(
            num_scalar_prefetch=1,
            grid=(count // npos,),
            in_specs=[
                pl.BlockSpec((1, nrad, 1, 1, sh, window), x_map(j)) for j in range(npos)
            ] + [
                pl.BlockSpec((npos, 8, window), lambda q, p: (q, 0, 0)),
                pl.BlockSpec((nr, 1), lambda q, p: (0, 0)),
                pl.BlockSpec((nr, 1), lambda q, p: (0, 0)),
                pl.BlockSpec((nr, 1), lambda q, p: (0, 0)),
                pl.BlockSpec((nr, nr), lambda q, p: (0, 0)),
                pl.BlockSpec((nr, nr), lambda q, p: (0, 0)),
            ],
            out_specs=pl.BlockSpec((nrad, 1, npos, sh, window), lambda q, p: (0, 0, q, 0, 0)),
            scratch_shapes=[pltpu.VMEM((nr + 2 * PAD, npos * window), jnp.float32)],
        ),
        compiler_params=pltpu.CompilerParams(vmem_limit_bytes=48 * 1024 * 1024),
        cost_estimate=pl.CostEstimate(
            flops=flops, transcendentals=0, bytes_accessed=4 * count * nr * window + 4 * nr * nr
        ),
    )(pos, *([x] * npos), info, kappa, invden, eig, dual_full, basis_full)


def unpack_kernel(r_ref, j_ref, ok_ref, x_ref, *refs):
    o_ref = refs[-1]
    nrad, window = x_ref.shape[0], x_ref.shape[-1]
    step = o_ref.shape[1]
    s = pl.program_id(0)
    for i in range(step):
        for w in range(nrad):
            k = (s * step + i) * nrad + w
            blk = x_ref[r_ref[k], 0, j_ref[k]]
            o_ref[0, i, :, w * window:(w + 1) * window] = jnp.where(
                ok_ref[k] > 0, blk, jnp.zeros_like(blk)
            )


def unpack(got, comp, comps, prev, src_r, src_j, src_ok, rows_here, step=8):
    nrad, _, count, sh, window = got.shape
    shape = (comps, rows_here, sh, nrad * window)
    in_specs = [pl.BlockSpec((nrad, 1, count, sh, window), lambda s, a, b, c: (0, 0, 0, 0, 0))]
    args = [got]
    aliases = {}
    if prev is not None:
        in_specs.append(pl.BlockSpec(memory_space=pl.ANY))
        args.append(prev)
        aliases = {4: 0}
    return pl.pallas_call(
        unpack_kernel,
        out_shape=jax.ShapeDtypeStruct(shape, got.dtype),
        grid_spec=pltpu.PrefetchScalarGridSpec(
            num_scalar_prefetch=3,
            grid=(rows_here // step,),
            in_specs=in_specs,
            out_specs=pl.BlockSpec(
                (1, step, sh, nrad * window), lambda s, a, b, c: (comp, s, 0, 0)
            ),
        ),
        input_output_aliases=aliases,
        compiler_params=pltpu.CompilerParams(vmem_limit_bytes=48 * 1024 * 1024),
    )(src_r, src_j, src_ok, *args)


def on_device(
    spectra, diffusivity, eigenvalues, radial_basis, dual_basis, degree_count, order_slot
):
    comps, rows_here, shells_here, slots_total = spectra.shape
    shells_total = diffusivity.shape[0]
    orders_total = degree_count.shape[0]
    groups = lax.axis_size("mode")
    nrad = lax.axis_size("rad")
    per_group = rows_here // groups
    window = slots_total // nrad
    me_mode = lax.axis_index("mode")
    me_rad = lax.axis_index("rad")
    tab = layout_tables(groups, nrad, rows_here, slots_total, orders_total)

    shifts = jnp.asarray([row[0] for row in tab["dest"]], jnp.int32)
    recvs = []
    for comp in range(comps):
        send = pack(spectra, order_slot, shifts, comp, groups, nrad, per_group)
        recvs.append(lax.all_to_all(send, ("mode", "rad"), 0, 0, tiled=True))

    pos = jnp.asarray(tab["pos"], jnp.int32)[me_rad]
    win = jnp.asarray(tab["win"], jnp.int32)[me_rad]
    ok = jnp.asarray(tab["ok"], jnp.int32)[me_rad]
    in_rows = jnp.take(order_slot, me_mode * rows_here + pos)
    orders = in_rows * slots_total // (2 * orders_total)
    slot_ids = win[:, None] * window + jnp.arange(window, dtype=jnp.int32)[None, :]
    degree = (orders[:, None] + slot_ids).astype(jnp.float32)
    live = (slot_ids < jnp.take(degree_count, in_rows)[:, None]) & (ok[:, None] > 0)
    count = tab["count"]
    info = jnp.zeros((count, 8, window), jnp.float32)
    info = info.at[:, 0, :].set(degree)
    info = info.at[:, 1, :].set(live.astype(jnp.float32))

    radius = 1.2 + jnp.arange(shells_total, dtype=jnp.int32).astype(jnp.float32) / shells_total
    invden = (1.0 / ((shells_total * radius) ** 2)).reshape(shells_total, 1)
    kappa = diffusivity.reshape(shells_total, 1)
    eig = eigenvalues.reshape(shells_total, 1)

    identity = jnp.eye(shells_total, dtype=jnp.float32)
    basis_full = (identity + radial_basis.astype(jnp.float32)).astype(jnp.bfloat16)
    dual_full = (identity + dual_basis.astype(jnp.float32)).astype(jnp.bfloat16)
    gots = []
    for recv in recvs:
        back = solve(recv, pos, info, kappa, invden, eig, dual_full, basis_full, groups, nrad,
                     per_group)
        gots.append(lax.all_to_all(back, "rad", 0, 0, tiled=True))
    src_r = jnp.asarray(tab["src_r"], jnp.int32)
    src_j = jnp.asarray(tab["src_j"], jnp.int32)
    src_ok = jnp.asarray(tab["src_ok"], jnp.int32)
    out = None
    for comp, got in enumerate(gots):
        out = unpack(got, comp, comps, out, src_r, src_j, src_ok, rows_here)
    return out


def solution(mesh):
    placed = (P(None, "mode", "rad", None), P(), P(), P(), P(), P(), P())
    return jax.shard_map(
        on_device,
        mesh=mesh,
        in_specs=placed,
        out_specs=P(None, "mode", "rad", None),
        check_vma=False,
    )
```

```python
import functools

import jax
import jax.numpy as jnp
from jax import lax
from jax.experimental import pallas as pl
from jax.experimental.pallas import tpu as pltpu
from jax.sharding import PartitionSpec as P

PAD = 8


def layout_tables(groups, nrad, rows_here, slots_total, orders_total):
    window = slots_total // nrad
    nwin = []
    for s in range(groups):
        least = (s * rows_here) * slots_total // (2 * orders_total)
        nwin.append(max(1, min(nrad, -(-(slots_total - least) // window))))
    load = [0] * nrad
    shift = [0] * groups
    for s in sorted(range(groups), key=lambda s: nwin[s]):
        best = None
        for sh in range(nrad):
            trial = load[:]
            for w in range(nwin[s], nrad):
                trial[(w + sh) % nrad] += 1
            key = (max(trial), sum(x * x for x in trial))
            if best is None or key < best[0]:
                best = (key, sh, trial)
        shift[s], load = best[1], best[2]
    lists = []
    for r in range(nrad):
        lists.append([s for s in range(groups) if (r - shift[s]) % nrad < nwin[s]])
    count = max(len(x) for x in lists)
    pos_tab, win_tab, ok_tab = [], [], []
    for r in range(nrad):
        entries = lists[r] + [lists[r][0]] * (count - len(lists[r]))
        pos_tab.append(entries)
        win_tab.append([(r - shift[s]) % nrad for s in entries])
        ok_tab.append([1] * len(lists[r]) + [0] * (count - len(lists[r])))
    src_r, src_j, src_ok = [], [], []
    for s in range(groups):
        for w in range(nrad):
            r = (w + shift[s]) % nrad
            live = w < nwin[s]
            src_r.append(r)
            src_j.append(lists[r].index(s) if live else 0)
            src_ok.append(1 if live else 0)
    dest_tab = [[(w + shift[s]) % nrad for w in range(nrad)] for s in range(groups)]
    return dict(count=count, pos=pos_tab, win=win_tab, ok=ok_tab, src_r=src_r, src_j=src_j,
                src_ok=src_ok, dest=dest_tab)


def pack_kernel(order_ref, shift_ref, *refs):
    x_refs, o_ref = refs[:-1], refs[-1]
    nrad, window = o_ref.shape[0] // len(x_refs), o_ref.shape[-1]
    turn = shift_ref[lax.axis_index("mode")]
    for i, x_ref in enumerate(x_refs):
        for w in range(nrad):
            o_ref[i * nrad + (w + turn) % nrad] = x_ref[:, 0:1, :, w * window:(w + 1) * window]


def pack(spectra, order_slot, shifts, comp, groups, nrad, per_group, step=16):
    comps, rows_here, shells_here, slots_total = spectra.shape
    window = slots_total // nrad
    picks_total = groups * per_group

    def in_map(i):
        def index(q, p, d):
            me = lax.axis_index("mode")
            return (comp, p[(q * step + i) * rows_here + me * per_group] - me * rows_here, 0, 0)

        return index

    def out_map(q, p, d):
        return (q, 0, 0, 0, 0)

    assert per_group == 1 and picks_total % step == 0
    return pl.pallas_call(
        pack_kernel,
        out_shape=jax.ShapeDtypeStruct(
            (groups * nrad, 1, per_group, shells_here, window), spectra.dtype
        ),
        grid_spec=pltpu.PrefetchScalarGridSpec(
            num_scalar_prefetch=2,
            grid=(picks_total // step,),
            in_specs=[
                pl.BlockSpec((1, 1, shells_here, slots_total), in_map(i))
                for i in range(step)
            ],
            out_specs=pl.BlockSpec((step * nrad, 1, per_group, shells_here, window), out_map),
        ),
    )(order_slot, shifts, *([spectra] * step))


def solve_kernel(pos_ref, *refs):
    npos = len(refs) - 8
    x_refs = refs[:npos]
    info_ref, kappa_ref, invden_ref, eig_ref, d_ref, b_ref, o_ref, pad_ref = refs[npos:]
    nrad = x_refs[0].shape[1]
    sh, window = x_refs[0].shape[4], x_refs[0].shape[5]
    nr = nrad * sh
    cols = [x_ref[0, :, 0, 0].reshape(nr, window) for x_ref in x_refs]
    f = jnp.concatenate(cols, axis=1).astype(jnp.float32)
    width = f.shape[1]
    pad_ref[0:PAD, :] = jnp.zeros((PAD, width), jnp.float32)
    pad_ref[PAD + nr:PAD + nr + PAD, :] = jnp.zeros((PAD, width), jnp.float32)
    pad_ref[PAD:PAD + nr, :] = f
    m2 = pad_ref[PAD - 2:PAD - 2 + nr, :]
    m1 = pad_ref[PAD - 1:PAD - 1 + nr, :]
    p1 = pad_ref[PAD + 1:PAD + 1 + nr, :]
    p2 = pad_ref[PAD + 2:PAD + 2 + nr, :]
    second = (-m2 + 16.0 * m1 - 30.0 * f + 16.0 * p1 - p2) / 12.0
    deg = jnp.concatenate([info_ref[j, 0:1, :] for j in range(npos)], axis=1)
    live = jnp.concatenate([info_ref[j, 1:2, :] for j in range(npos)], axis=1) > 0.5
    lterm = deg * (deg + 1.0)
    damping = lterm * invden_ref[...]
    updated = f + 0.5 * kappa_ref[...] * (second - damping * f)
    updated = jnp.where(live, updated, 0.0).astype(jnp.bfloat16)
    projected = jnp.dot(d_ref[...], updated, preferred_element_type=jnp.float32)
    divisor = eig_ref[...] + 0.5 * lterm / float(nr * nr)
    scaled = (projected / divisor).astype(jnp.bfloat16)
    restored = jnp.dot(b_ref[...], scaled, preferred_element_type=jnp.float32)
    solved = jnp.where(live, restored, 0.0).astype(jnp.bfloat16)
    for j in range(npos):
        o_ref[:, 0, j] = solved[:, j * window:(j + 1) * window].reshape(nrad, sh, window)


def solve(recv, pos, info, kappa, invden, eig, dual_full, basis_full, groups, nrad, per_group,
          npos=1):
    _, _, _, sh, window = recv.shape
    nr = nrad * sh
    count = pos.shape[0]
    assert per_group == 1 and count % npos == 0
    x = recv.reshape(groups, nrad, 1, per_group, sh, window)
    flops = 2 * 2 * nr * nr * window * count

    def x_map(j):
        return lambda q, p: (p[q * npos + j], 0, 0, 0, 0, 0)

    return pl.pallas_call(
        solve_kernel,
        out_shape=jax.ShapeDtypeStruct((nrad, 1, count, sh, window), jnp.bfloat16),
        grid_spec=pltpu.PrefetchScalarGridSpec(
            num_scalar_prefetch=1,
            grid=(count // npos,),
            in_specs=[
                pl.BlockSpec((1, nrad, 1, 1, sh, window), x_map(j)) for j in range(npos)
            ] + [
                pl.BlockSpec((npos, 8, window), lambda q, p: (q, 0, 0)),
                pl.BlockSpec((nr, 1), lambda q, p: (0, 0)),
                pl.BlockSpec((nr, 1), lambda q, p: (0, 0)),
                pl.BlockSpec((nr, 1), lambda q, p: (0, 0)),
                pl.BlockSpec((nr, nr), lambda q, p: (0, 0)),
                pl.BlockSpec((nr, nr), lambda q, p: (0, 0)),
            ],
            out_specs=pl.BlockSpec((nrad, 1, npos, sh, window), lambda q, p: (0, 0, q, 0, 0)),
            scratch_shapes=[pltpu.VMEM((nr + 2 * PAD, npos * window), jnp.float32)],
        ),
        compiler_params=pltpu.CompilerParams(vmem_limit_bytes=48 * 1024 * 1024),
        cost_estimate=pl.CostEstimate(
            flops=flops, transcendentals=0, bytes_accessed=4 * count * nr * window + 4 * nr * nr
        ),
    )(pos, *([x] * npos), info, kappa, invden, eig, dual_full, basis_full)


def unpack_kernel(r_ref, j_ref, ok_ref, x_ref, *refs):
    o_ref = refs[-1]
    nrad, window = x_ref.shape[0], x_ref.shape[-1]
    step = o_ref.shape[1]
    s = pl.program_id(0)
    for i in range(step):
        for w in range(nrad):
            k = (s * step + i) * nrad + w
            blk = x_ref[r_ref[k], 0, j_ref[k]]
            o_ref[0, i, :, w * window:(w + 1) * window] = jnp.where(
                ok_ref[k] > 0, blk, jnp.zeros_like(blk)
            )


def unpack(got, comp, comps, prev, src_r, src_j, src_ok, rows_here, step=16):
    nrad, _, count, sh, window = got.shape
    shape = (comps, rows_here, sh, nrad * window)
    in_specs = [pl.BlockSpec((nrad, 1, count, sh, window), lambda s, a, b, c: (0, 0, 0, 0, 0))]
    args = [got]
    aliases = {}
    if prev is not None:
        in_specs.append(pl.BlockSpec(memory_space=pl.ANY))
        args.append(prev)
        aliases = {4: 0}
    return pl.pallas_call(
        unpack_kernel,
        out_shape=jax.ShapeDtypeStruct(shape, got.dtype),
        grid_spec=pltpu.PrefetchScalarGridSpec(
            num_scalar_prefetch=3,
            grid=(rows_here // step,),
            in_specs=in_specs,
            out_specs=pl.BlockSpec(
                (1, step, sh, nrad * window), lambda s, a, b, c: (comp, s, 0, 0)
            ),
        ),
        input_output_aliases=aliases,
        compiler_params=pltpu.CompilerParams(vmem_limit_bytes=48 * 1024 * 1024),
    )(src_r, src_j, src_ok, *args)


def on_device(
    spectra, diffusivity, eigenvalues, radial_basis, dual_basis, degree_count, order_slot
):
    comps, rows_here, shells_here, slots_total = spectra.shape
    shells_total = diffusivity.shape[0]
    orders_total = degree_count.shape[0]
    groups = lax.axis_size("mode")
    nrad = lax.axis_size("rad")
    per_group = rows_here // groups
    window = slots_total // nrad
    me_mode = lax.axis_index("mode")
    me_rad = lax.axis_index("rad")
    tab = layout_tables(groups, nrad, rows_here, slots_total, orders_total)

    shifts = jnp.asarray([row[0] for row in tab["dest"]], jnp.int32)
    recvs = []
    for comp in range(comps):
        send = pack(spectra, order_slot, shifts, comp, groups, nrad, per_group)
        recvs.append(lax.all_to_all(send, ("mode", "rad"), 0, 0, tiled=True))

    pos = jnp.asarray(tab["pos"], jnp.int32)[me_rad]
    win = jnp.asarray(tab["win"], jnp.int32)[me_rad]
    ok = jnp.asarray(tab["ok"], jnp.int32)[me_rad]
    in_rows = jnp.take(order_slot, me_mode * rows_here + pos)
    orders = in_rows * slots_total // (2 * orders_total)
    slot_ids = win[:, None] * window + jnp.arange(window, dtype=jnp.int32)[None, :]
    degree = (orders[:, None] + slot_ids).astype(jnp.float32)
    live = (slot_ids < jnp.take(degree_count, in_rows)[:, None]) & (ok[:, None] > 0)
    count = tab["count"]
    info = jnp.zeros((count, 8, window), jnp.float32)
    info = info.at[:, 0, :].set(degree)
    info = info.at[:, 1, :].set(live.astype(jnp.float32))

    radius = 1.2 + jnp.arange(shells_total, dtype=jnp.int32).astype(jnp.float32) / shells_total
    invden = (1.0 / ((shells_total * radius) ** 2)).reshape(shells_total, 1)
    kappa = diffusivity.reshape(shells_total, 1)
    eig = eigenvalues.reshape(shells_total, 1)

    identity = jnp.eye(shells_total, dtype=jnp.float32)
    basis_full = (identity + radial_basis.astype(jnp.float32)).astype(jnp.bfloat16)
    dual_full = (identity + dual_basis.astype(jnp.float32)).astype(jnp.bfloat16)
    gots = []
    for recv in recvs:
        back = solve(recv, pos, info, kappa, invden, eig, dual_full, basis_full, groups, nrad,
                     per_group)
        gots.append(lax.all_to_all(back, "rad", 0, 0, tiled=True))
    src_r = jnp.asarray(tab["src_r"], jnp.int32)
    src_j = jnp.asarray(tab["src_j"], jnp.int32)
    src_ok = jnp.asarray(tab["src_ok"], jnp.int32)
    out = None
    for comp, got in enumerate(gots):
        out = unpack(got, comp, comps, out, src_r, src_j, src_ok, rows_here)
    return out


def solution(mesh):
    placed = (P(None, "mode", "rad", None), P(), P(), P(), P(), P(), P())
    return jax.shard_map(
        on_device,
        mesh=mesh,
        in_specs=placed,
        out_specs=P(None, "mode", "rad", None),
        check_vma=False,
    )
```

```python
import functools

import jax
import jax.numpy as jnp
from jax import lax
from jax.experimental import pallas as pl
from jax.experimental.pallas import tpu as pltpu
from jax.sharding import PartitionSpec as P

PAD = 8


def layout_tables(groups, nrad, rows_here, slots_total, orders_total):
    window = slots_total // nrad
    nwin = []
    for s in range(groups):
        least = (s * rows_here) * slots_total // (2 * orders_total)
        nwin.append(max(1, min(nrad, -(-(slots_total - least) // window))))
    load = [0] * nrad
    shift = [0] * groups
    for s in sorted(range(groups), key=lambda s: nwin[s]):
        best = None
        for sh in range(nrad):
            trial = load[:]
            for w in range(nwin[s], nrad):
                trial[(w + sh) % nrad] += 1
            key = (max(trial), sum(x * x for x in trial))
            if best is None or key < best[0]:
                best = (key, sh, trial)
        shift[s], load = best[1], best[2]
    lists = []
    for r in range(nrad):
        lists.append([s for s in range(groups) if (r - shift[s]) % nrad < nwin[s]])
    count = max(len(x) for x in lists)
    pos_tab, win_tab, ok_tab = [], [], []
    for r in range(nrad):
        entries = lists[r] + [lists[r][0]] * (count - len(lists[r]))
        pos_tab.append(entries)
        win_tab.append([(r - shift[s]) % nrad for s in entries])
        ok_tab.append([1] * len(lists[r]) + [0] * (count - len(lists[r])))
    src_r, src_j, src_ok = [], [], []
    for s in range(groups):
        for w in range(nrad):
            r = (w + shift[s]) % nrad
            live = w < nwin[s]
            src_r.append(r)
            src_j.append(lists[r].index(s) if live else 0)
            src_ok.append(1 if live else 0)
    dest_tab = [[(w + shift[s]) % nrad for w in range(nrad)] for s in range(groups)]
    return dict(count=count, pos=pos_tab, win=win_tab, ok=ok_tab, src_r=src_r, src_j=src_j,
                src_ok=src_ok, dest=dest_tab)


def pack_kernel(order_ref, shift_ref, *refs):
    x_refs, o_ref = refs[:-1], refs[-1]
    nrad, window = o_ref.shape[0], o_ref.shape[-1]
    turn = shift_ref[lax.axis_index("mode")]
    for i, x_ref in enumerate(x_refs):
        for w in range(nrad):
            o_ref[(w + turn) % nrad, i] = x_ref[:, 0:1, :, w * window:(w + 1) * window]


def pack(spectra, order_slot, shifts, comp, groups, nrad, per_group, step=8):
    comps, rows_here, shells_here, slots_total = spectra.shape
    window = slots_total // nrad
    picks_total = groups * per_group

    def in_map(i):
        def index(q, p, d):
            me = lax.axis_index("mode")
            return (comp, p[(q * step + i) * rows_here + me * per_group] - me * rows_here, 0, 0)

        return index

    def out_map(q, p, d):
        return (0, q, 0, 0, 0, 0)

    assert per_group == 1 and picks_total % step == 0
    return pl.pallas_call(
        pack_kernel,
        out_shape=jax.ShapeDtypeStruct(
            (nrad, groups, 1, per_group, shells_here, window), spectra.dtype
        ),
        grid_spec=pltpu.PrefetchScalarGridSpec(
            num_scalar_prefetch=2,
            grid=(picks_total // step,),
            in_specs=[
                pl.BlockSpec((1, 1, shells_here, slots_total), in_map(i))
                for i in range(step)
            ],
            out_specs=pl.BlockSpec((nrad, step, 1, per_group, shells_here, window), out_map),
        ),
    )(order_slot, shifts, *([spectra] * step))


def solve_kernel(pos_ref, *refs):
    npos = len(refs) - 8
    x_refs = refs[:npos]
    info_ref, kappa_ref, invden_ref, eig_ref, d_ref, b_ref, o_ref, pad_ref = refs[npos:]
    nrad = x_refs[0].shape[0]
    sh, window = x_refs[0].shape[4], x_refs[0].shape[5]
    nr = nrad * sh
    cols = [x_ref[:, 0, 0, 0].reshape(nr, window) for x_ref in x_refs]
    f = jnp.concatenate(cols, axis=1).astype(jnp.float32)
    width = f.shape[1]
    pad_ref[0:PAD, :] = jnp.zeros((PAD, width), jnp.float32)
    pad_ref[PAD + nr:PAD + nr + PAD, :] = jnp.zeros((PAD, width), jnp.float32)
    pad_ref[PAD:PAD + nr, :] = f
    m2 = pad_ref[PAD - 2:PAD - 2 + nr, :]
    m1 = pad_ref[PAD - 1:PAD - 1 + nr, :]
    p1 = pad_ref[PAD + 1:PAD + 1 + nr, :]
    p2 = pad_ref[PAD + 2:PAD + 2 + nr, :]
    second = (-m2 + 16.0 * m1 - 30.0 * f + 16.0 * p1 - p2) / 12.0
    deg = jnp.concatenate([info_ref[j, 0:1, :] for j in range(npos)], axis=1)
    live = jnp.concatenate([info_ref[j, 1:2, :] for j in range(npos)], axis=1) > 0.5
    lterm = deg * (deg + 1.0)
    damping = lterm * invden_ref[...]
    updated = f + 0.5 * kappa_ref[...] * (second - damping * f)
    updated = jnp.where(live, updated, 0.0).astype(jnp.bfloat16)
    projected = jnp.dot(d_ref[...], updated, preferred_element_type=jnp.float32)
    divisor = eig_ref[...] + 0.5 * lterm / float(nr * nr)
    scaled = (projected / divisor).astype(jnp.bfloat16)
    restored = jnp.dot(b_ref[...], scaled, preferred_element_type=jnp.float32)
    solved = jnp.where(live, restored, 0.0).astype(jnp.bfloat16)
    for j in range(npos):
        o_ref[:, 0, j] = solved[:, j * window:(j + 1) * window].reshape(nrad, sh, window)


def solve(recv, pos, info, kappa, invden, eig, dual_full, basis_full, groups, nrad, per_group,
          npos=1):
    _, _, _, sh, window = recv.shape
    nr = nrad * sh
    count = pos.shape[0]
    assert per_group == 1 and count % npos == 0
    x = recv.reshape(nrad, groups, 1, per_group, sh, window)
    flops = 2 * 2 * nr * nr * window * count

    def x_map(j):
        return lambda q, p: (0, p[q * npos + j], 0, 0, 0, 0)

    return pl.pallas_call(
        solve_kernel,
        out_shape=jax.ShapeDtypeStruct((nrad, 1, count, sh, window), jnp.bfloat16),
        grid_spec=pltpu.PrefetchScalarGridSpec(
            num_scalar_prefetch=1,
            grid=(count // npos,),
            in_specs=[
                pl.BlockSpec((nrad, 1, 1, 1, sh, window), x_map(j)) for j in range(npos)
            ] + [
                pl.BlockSpec((npos, 8, window), lambda q, p: (q, 0, 0)),
                pl.BlockSpec((nr, 1), lambda q, p: (0, 0)),
                pl.BlockSpec((nr, 1), lambda q, p: (0, 0)),
                pl.BlockSpec((nr, 1), lambda q, p: (0, 0)),
                pl.BlockSpec((nr, nr), lambda q, p: (0, 0)),
                pl.BlockSpec((nr, nr), lambda q, p: (0, 0)),
            ],
            out_specs=pl.BlockSpec((nrad, 1, npos, sh, window), lambda q, p: (0, 0, q, 0, 0)),
            scratch_shapes=[pltpu.VMEM((nr + 2 * PAD, npos * window), jnp.float32)],
        ),
        compiler_params=pltpu.CompilerParams(vmem_limit_bytes=48 * 1024 * 1024),
        cost_estimate=pl.CostEstimate(
            flops=flops, transcendentals=0, bytes_accessed=4 * count * nr * window + 4 * nr * nr
        ),
    )(pos, *([x] * npos), info, kappa, invden, eig, dual_full, basis_full)


def unpack_kernel(r_ref, j_ref, ok_ref, x_ref, *refs):
    o_ref = refs[-1]
    nrad, window = x_ref.shape[0], x_ref.shape[-1]
    step = o_ref.shape[1]
    s = pl.program_id(0)
    for i in range(step):
        for w in range(nrad):
            k = (s * step + i) * nrad + w
            blk = x_ref[r_ref[k], 0, j_ref[k]]
            o_ref[0, i, :, w * window:(w + 1) * window] = jnp.where(
                ok_ref[k] > 0, blk, jnp.zeros_like(blk)
            )


def unpack(got, comp, comps, prev, src_r, src_j, src_ok, rows_here, step=8):
    nrad, _, count, sh, window = got.shape
    shape = (comps, rows_here, sh, nrad * window)
    in_specs = [pl.BlockSpec((nrad, 1, count, sh, window), lambda s, a, b, c: (0, 0, 0, 0, 0))]
    args = [got]
    aliases = {}
    if prev is not None:
        in_specs.append(pl.BlockSpec(memory_space=pl.ANY))
        args.append(prev)
        aliases = {4: 0}
    return pl.pallas_call(
        unpack_kernel,
        out_shape=jax.ShapeDtypeStruct(shape, got.dtype),
        grid_spec=pltpu.PrefetchScalarGridSpec(
            num_scalar_prefetch=3,
            grid=(rows_here // step,),
            in_specs=in_specs,
            out_specs=pl.BlockSpec(
                (1, step, sh, nrad * window), lambda s, a, b, c: (comp, s, 0, 0)
            ),
        ),
        input_output_aliases=aliases,
        compiler_params=pltpu.CompilerParams(vmem_limit_bytes=48 * 1024 * 1024),
    )(src_r, src_j, src_ok, *args)


def on_device(
    spectra, diffusivity, eigenvalues, radial_basis, dual_basis, degree_count, order_slot
):
    comps, rows_here, shells_here, slots_total = spectra.shape
    shells_total = diffusivity.shape[0]
    orders_total = degree_count.shape[0]
    groups = lax.axis_size("mode")
    nrad = lax.axis_size("rad")
    per_group = rows_here // groups
    window = slots_total // nrad
    me_mode = lax.axis_index("mode")
    me_rad = lax.axis_index("rad")
    tab = layout_tables(groups, nrad, rows_here, slots_total, orders_total)

    shifts = jnp.asarray([row[0] for row in tab["dest"]], jnp.int32)
    recvs = []
    for comp in range(comps):
        send = pack(spectra, order_slot, shifts, comp, groups, nrad, per_group)
        send = send.reshape((nrad * groups,) + send.shape[2:])
        recvs.append(lax.all_to_all(send, ("rad", "mode"), 0, 0, tiled=True))

    pos = jnp.asarray(tab["pos"], jnp.int32)[me_rad]
    win = jnp.asarray(tab["win"], jnp.int32)[me_rad]
    ok = jnp.asarray(tab["ok"], jnp.int32)[me_rad]
    in_rows = jnp.take(order_slot, me_mode * rows_here + pos)
    orders = in_rows * slots_total // (2 * orders_total)
    slot_ids = win[:, None] * window + jnp.arange(window, dtype=jnp.int32)[None, :]
    degree = (orders[:, None] + slot_ids).astype(jnp.float32)
    live = (slot_ids < jnp.take(degree_count, in_rows)[:, None]) & (ok[:, None] > 0)
    count = tab["count"]
    info = jnp.zeros((count, 8, window), jnp.float32)
    info = info.at[:, 0, :].set(degree)
    info = info.at[:, 1, :].set(live.astype(jnp.float32))

    radius = 1.2 + jnp.arange(shells_total, dtype=jnp.int32).astype(jnp.float32) / shells_total
    invden = (1.0 / ((shells_total * radius) ** 2)).reshape(shells_total, 1)
    kappa = diffusivity.reshape(shells_total, 1)
    eig = eigenvalues.reshape(shells_total, 1)

    identity = jnp.eye(shells_total, dtype=jnp.float32)
    basis_full = (identity + radial_basis.astype(jnp.float32)).astype(jnp.bfloat16)
    dual_full = (identity + dual_basis.astype(jnp.float32)).astype(jnp.bfloat16)
    gots = []
    for recv in recvs:
        back = solve(recv, pos, info, kappa, invden, eig, dual_full, basis_full, groups, nrad,
                     per_group)
        gots.append(lax.all_to_all(back, "rad", 0, 0, tiled=True))
    src_r = jnp.asarray(tab["src_r"], jnp.int32)
    src_j = jnp.asarray(tab["src_j"], jnp.int32)
    src_ok = jnp.asarray(tab["src_ok"], jnp.int32)
    out = None
    for comp, got in enumerate(gots):
        out = unpack(got, comp, comps, out, src_r, src_j, src_ok, rows_here)
    return out


def solution(mesh):
    placed = (P(None, "mode", "rad", None), P(), P(), P(), P(), P(), P())
    return jax.shard_map(
        on_device,
        mesh=mesh,
        in_specs=placed,
        out_specs=P(None, "mode", "rad", None),
        check_vma=False,
    )
```

```python
import functools

import jax
import jax.numpy as jnp
from jax import lax
from jax.experimental import pallas as pl
from jax.experimental.pallas import tpu as pltpu
from jax.sharding import PartitionSpec as P

PAD = 8


def layout_tables(groups, nrad, rows_here, slots_total, orders_total):
    window = slots_total // nrad
    nwin = []
    for s in range(groups):
        least = (s * rows_here) * slots_total // (2 * orders_total)
        nwin.append(max(1, min(nrad, -(-(slots_total - least) // window))))
    load = [0] * nrad
    shift = [0] * groups
    for s in sorted(range(groups), key=lambda s: nwin[s]):
        best = None
        for sh in range(nrad):
            trial = load[:]
            for w in range(nwin[s], nrad):
                trial[(w + sh) % nrad] += 1
            key = (max(trial), sum(x * x for x in trial))
            if best is None or key < best[0]:
                best = (key, sh, trial)
        shift[s], load = best[1], best[2]
    lists = []
    for r in range(nrad):
        lists.append([s for s in range(groups) if (r - shift[s]) % nrad < nwin[s]])
    count = max(len(x) for x in lists)
    pos_tab, win_tab, ok_tab = [], [], []
    for r in range(nrad):
        entries = lists[r] + [lists[r][0]] * (count - len(lists[r]))
        pos_tab.append(entries)
        win_tab.append([(r - shift[s]) % nrad for s in entries])
        ok_tab.append([1] * len(lists[r]) + [0] * (count - len(lists[r])))
    src_r, src_j, src_ok = [], [], []
    for s in range(groups):
        for w in range(nrad):
            r = (w + shift[s]) % nrad
            live = w < nwin[s]
            src_r.append(r)
            src_j.append(lists[r].index(s) if live else 0)
            src_ok.append(1 if live else 0)
    dest_tab = [[(w + shift[s]) % nrad for w in range(nrad)] for s in range(groups)]
    return dict(count=count, pos=pos_tab, win=win_tab, ok=ok_tab, src_r=src_r, src_j=src_j,
                src_ok=src_ok, dest=dest_tab)


def pack_kernel(order_ref, shift_ref, *refs):
    x_refs, o_ref = refs[:-1], refs[-1]
    nrad, window = o_ref.shape[0], o_ref.shape[-1]
    turn = shift_ref[lax.axis_index("mode")]
    for i, x_ref in enumerate(x_refs):
        for w in range(nrad):
            o_ref[(w + turn) % nrad, i] = x_ref[:, 0:1, :, w * window:(w + 1) * window]


def pack(spectra, order_slot, shifts, comp, groups, nrad, per_group, step=8):
    comps, rows_here, shells_here, slots_total = spectra.shape
    window = slots_total // nrad
    picks_total = groups * per_group

    def in_map(i):
        def index(q, p, d):
            me = lax.axis_index("mode")
            return (comp, p[(q * step + i) * rows_here + me * per_group] - me * rows_here, 0, 0)

        return index

    def out_map(q, p, d):
        return (0, q, 0, 0, 0, 0)

    assert per_group == 1 and picks_total % step == 0
    return pl.pallas_call(
        pack_kernel,
        out_shape=jax.ShapeDtypeStruct(
            (nrad, groups, 1, per_group, shells_here, window), spectra.dtype
        ),
        grid_spec=pltpu.PrefetchScalarGridSpec(
            num_scalar_prefetch=2,
            grid=(picks_total // step,),
            in_specs=[
                pl.BlockSpec((1, 1, shells_here, slots_total), in_map(i))
                for i in range(step)
            ],
            out_specs=pl.BlockSpec((nrad, step, 1, per_group, shells_here, window), out_map),
        ),
    )(order_slot, shifts, *([spectra] * step))


def solve_kernel(pos_ref, *refs):
    npos = len(refs) - 6
    x_refs = refs[:npos]
    info_ref, shell_ref, d_ref, b_ref, o_ref, pad_ref = refs[npos:]
    kappa = shell_ref[:, 0:1]
    invden = shell_ref[:, 1:2]
    eig = shell_ref[:, 2:3]
    nrad = x_refs[0].shape[0]
    sh, window = x_refs[0].shape[4], x_refs[0].shape[5]
    nr = nrad * sh
    cols = [x_ref[:, 0, 0, 0].reshape(nr, window) for x_ref in x_refs]
    f = jnp.concatenate(cols, axis=1).astype(jnp.float32)
    width = f.shape[1]
    pad_ref[0:PAD, :] = jnp.zeros((PAD, width), jnp.float32)
    pad_ref[PAD + nr:PAD + nr + PAD, :] = jnp.zeros((PAD, width), jnp.float32)
    pad_ref[PAD:PAD + nr, :] = f
    m2 = pad_ref[PAD - 2:PAD - 2 + nr, :]
    m1 = pad_ref[PAD - 1:PAD - 1 + nr, :]
    p1 = pad_ref[PAD + 1:PAD + 1 + nr, :]
    p2 = pad_ref[PAD + 2:PAD + 2 + nr, :]
    second = (-m2 + 16.0 * m1 - 30.0 * f + 16.0 * p1 - p2) / 12.0
    deg = jnp.concatenate([info_ref[j, 0:1, :] for j in range(npos)], axis=1)
    live = jnp.concatenate([info_ref[j, 1:2, :] for j in range(npos)], axis=1) > 0.5
    lterm = deg * (deg + 1.0)
    damping = lterm * invden
    updated = f + 0.5 * kappa * (second - damping * f)
    updated = jnp.where(live, updated, 0.0).astype(jnp.bfloat16)
    projected = jnp.dot(d_ref[...], updated, preferred_element_type=jnp.float32)
    divisor = eig + 0.5 * lterm / float(nr * nr)
    scaled = (projected / divisor).astype(jnp.bfloat16)
    restored = jnp.dot(b_ref[...], scaled, preferred_element_type=jnp.float32)
    solved = jnp.where(live, restored, 0.0).astype(jnp.bfloat16)
    for j in range(npos):
        o_ref[:, 0, j] = solved[:, j * window:(j + 1) * window].reshape(nrad, sh, window)


def solve(recv, pos, info, shell, dual_full, basis_full, groups, nrad, per_group,
          npos=1):
    _, _, _, sh, window = recv.shape
    nr = nrad * sh
    count = pos.shape[0]
    assert per_group == 1 and count % npos == 0
    x = recv.reshape(nrad, groups, 1, per_group, sh, window)
    flops = 2 * 2 * nr * nr * window * count

    def x_map(j):
        return lambda q, p: (0, p[q * npos + j], 0, 0, 0, 0)

    return pl.pallas_call(
        solve_kernel,
        out_shape=jax.ShapeDtypeStruct((nrad, 1, count, sh, window), jnp.bfloat16),
        grid_spec=pltpu.PrefetchScalarGridSpec(
            num_scalar_prefetch=1,
            grid=(count // npos,),
            in_specs=[
                pl.BlockSpec((nrad, 1, 1, 1, sh, window), x_map(j)) for j in range(npos)
            ] + [
                pl.BlockSpec((npos, 8, window), lambda q, p: (q, 0, 0)),
                pl.BlockSpec((nr, 3), lambda q, p: (0, 0)),
                pl.BlockSpec((nr, nr), lambda q, p: (0, 0)),
                pl.BlockSpec((nr, nr), lambda q, p: (0, 0)),
            ],
            out_specs=pl.BlockSpec((nrad, 1, npos, sh, window), lambda q, p: (0, 0, q, 0, 0)),
            scratch_shapes=[pltpu.VMEM((nr + 2 * PAD, npos * window), jnp.float32)],
        ),
        compiler_params=pltpu.CompilerParams(vmem_limit_bytes=48 * 1024 * 1024),
        cost_estimate=pl.CostEstimate(
            flops=flops, transcendentals=0, bytes_accessed=4 * count * nr * window + 4 * nr * nr
        ),
    )(pos, *([x] * npos), info, shell, dual_full, basis_full)


def unpack_kernel(r_ref, j_ref, ok_ref, x_ref, *refs):
    o_ref = refs[-1]
    nrad, window = x_ref.shape[0], x_ref.shape[-1]
    step = o_ref.shape[1]
    s = pl.program_id(0)
    for i in range(step):
        for w in range(nrad):
            k = (s * step + i) * nrad + w
            blk = x_ref[r_ref[k], 0, j_ref[k]]
            o_ref[0, i, :, w * window:(w + 1) * window] = jnp.where(
                ok_ref[k] > 0, blk, jnp.zeros_like(blk)
            )


def unpack(got, comp, comps, prev, src_r, src_j, src_ok, rows_here, step=8):
    nrad, _, count, sh, window = got.shape
    shape = (comps, rows_here, sh, nrad * window)
    in_specs = [pl.BlockSpec((nrad, 1, count, sh, window), lambda s, a, b, c: (0, 0, 0, 0, 0))]
    args = [got]
    aliases = {}
    if prev is not None:
        in_specs.append(pl.BlockSpec(memory_space=pl.ANY))
        args.append(prev)
        aliases = {4: 0}
    return pl.pallas_call(
        unpack_kernel,
        out_shape=jax.ShapeDtypeStruct(shape, got.dtype),
        grid_spec=pltpu.PrefetchScalarGridSpec(
            num_scalar_prefetch=3,
            grid=(rows_here // step,),
            in_specs=in_specs,
            out_specs=pl.BlockSpec(
                (1, step, sh, nrad * window), lambda s, a, b, c: (comp, s, 0, 0)
            ),
        ),
        input_output_aliases=aliases,
        compiler_params=pltpu.CompilerParams(vmem_limit_bytes=48 * 1024 * 1024),
    )(src_r, src_j, src_ok, *args)


def on_device(
    spectra, diffusivity, eigenvalues, radial_basis, dual_basis, degree_count, order_slot
):
    comps, rows_here, shells_here, slots_total = spectra.shape
    shells_total = diffusivity.shape[0]
    orders_total = degree_count.shape[0]
    groups = lax.axis_size("mode")
    nrad = lax.axis_size("rad")
    per_group = rows_here // groups
    window = slots_total // nrad
    me_mode = lax.axis_index("mode")
    me_rad = lax.axis_index("rad")
    tab = layout_tables(groups, nrad, rows_here, slots_total, orders_total)

    shifts = jnp.asarray([row[0] for row in tab["dest"]], jnp.int32)
    recvs = []
    for comp in range(comps):
        send = pack(spectra, order_slot, shifts, comp, groups, nrad, per_group)
        send = send.reshape((nrad * groups,) + send.shape[2:])
        recvs.append(lax.all_to_all(send, ("rad", "mode"), 0, 0, tiled=True))

    pos = jnp.asarray(tab["pos"], jnp.int32)[me_rad]
    win = jnp.asarray(tab["win"], jnp.int32)[me_rad]
    ok = jnp.asarray(tab["ok"], jnp.int32)[me_rad]
    in_rows = jnp.take(order_slot, me_mode * rows_here + pos)
    orders = in_rows * slots_total // (2 * orders_total)
    slot_ids = win[:, None] * window + jnp.arange(window, dtype=jnp.int32)[None, :]
    degree = (orders[:, None] + slot_ids).astype(jnp.float32)
    live = (slot_ids < jnp.take(degree_count, in_rows)[:, None]) & (ok[:, None] > 0)
    count = tab["count"]
    info = jnp.zeros((count, 8, window), jnp.float32)
    info = info.at[:, 0, :].set(degree)
    info = info.at[:, 1, :].set(live.astype(jnp.float32))

    radius = 1.2 + jnp.arange(shells_total, dtype=jnp.int32).astype(jnp.float32) / shells_total
    invden = (1.0 / ((shells_total * radius) ** 2)).reshape(shells_total, 1)
    kappa = diffusivity.reshape(shells_total, 1)
    eig = eigenvalues.reshape(shells_total, 1)
    shell = jnp.concatenate([kappa, invden, eig], axis=1)

    identity = jnp.eye(shells_total, dtype=jnp.float32)
    basis_full = (identity + radial_basis.astype(jnp.float32)).astype(jnp.bfloat16)
    dual_full = (identity + dual_basis.astype(jnp.float32)).astype(jnp.bfloat16)
    gots = []
    for recv in recvs:
        back = solve(recv, pos, info, shell, dual_full, basis_full, groups, nrad,
                     per_group)
        gots.append(lax.all_to_all(back, "rad", 0, 0, tiled=True))
    src_r = jnp.asarray(tab["src_r"], jnp.int32)
    src_j = jnp.asarray(tab["src_j"], jnp.int32)
    src_ok = jnp.asarray(tab["src_ok"], jnp.int32)
    out = None
    for comp, got in enumerate(gots):
        out = unpack(got, comp, comps, out, src_r, src_j, src_ok, rows_here)
    return out


def solution(mesh):
    placed = (P(None, "mode", "rad", None), P(), P(), P(), P(), P(), P())
    return jax.shard_map(
        on_device,
        mesh=mesh,
        in_specs=placed,
        out_specs=P(None, "mode", "rad", None),
        check_vma=False,
    )
```
